256 devices in a mesh: group: 4 (over y), key: 64 (over z, x, core).
Axes of the slice: x: 4, y: 4, z: 8, core: 2. Of those that a mesh axis runs over, the one named last changes fastest.
Arguments:
- src_desc: bfloat16 [65536, 256], P(('group', 'key'))
- tgt_desc: bfloat16 [131072, 256], P('key')
- src_weight: float32 [65536], P(('group', 'key')), may hold values from 0.05 to 20
- tgt_weight: float32 [131072], P('key'), may hold values from 0.05 to 20
- tgt_dual: float32 [131072], P('key'), may hold values from -1.2 to 1.2
- pair_blocks: int32 [4, 64, 2, 64], P('group', 'key'), may hold values from 0 to 63, as said below
- pair_count: int32 [4, 64], P('group', 'key'), may hold values from 8 to 64, as said below
Outputs:
- src_dual: float32 [65536], P(('group', 'key'))
- tgt_dual_new: float32 [131072], P('key')
The draws below stay inside these ranges and needn't reach their ends.
Inputs may be any that keep to these rules, and one draw needn't show every extreme that they name: `pair_blocks`: row 0 holds source clusters 0 to 63, row 1 target clusters 0 to 7; the live slots of one device are distinct pairs; every source cluster and every target cluster is in some live pair. `pair_count`: live slots come first.
All inputs are finite; a program needn't handle non-finite values.
Results may differ from the reference program's by a relative error of at most 0.0003.
Values may be sent and summed in bfloat16 or wider, within the bound.
No kernel may reach another device: no remote copies, remote signals or barrier semaphores. Data moves between devices by JAX's collectives and lax.ppermute only.
A program may use at most 64 MiB of HBM per device.

```python
import math
import jax
import jax.numpy as jnp
from jax import lax

CLUSTER = 256
DESC = 256
TC_DEV = 8
SC_DEV = 1
PAIRS = 64
GROUPS = 4
KEYS = 64
SG = 64
NS = 65536
NT = 131072


def descriptor_draw(key, rows):
    return jax.random.normal(key, (rows, DESC), jnp.float32).astype(jnp.bfloat16)


def draw_src_desc(key, part):
    return descriptor_draw(jax.random.fold_in(key, 11), NS)


def draw_tgt_desc(key, part):
    return descriptor_draw(jax.random.fold_in(key, 13), NT)


def device_pairs(key, device):
    key_index = device % KEYS
    combos = SG * TC_DEV
    ranks = jax.random.permutation(jax.random.fold_in(key, device), combos).astype(jnp.int32)
    combo_ids = jnp.arange(combos, dtype=jnp.int32)
    src_ids = combo_ids // TC_DEV
    tgt_ids = combo_ids % TC_DEV
    anchor = src_ids == (key_index * SC_DEV + tgt_ids) % SG
    priority = jnp.where(anchor, tgt_ids - combos, ranks)
    order = jnp.argsort(priority, stable=True)[:PAIRS].astype(jnp.int32)
    return jnp.stack([order // TC_DEV, order % TC_DEV], axis=0)


def draw_pair_blocks(key, part):
    base = jax.random.fold_in(key, 17)
    devices_all = jnp.arange(GROUPS * KEYS, dtype=jnp.int32)
    lists = jax.vmap(lambda device: device_pairs(base, device))(devices_all)
    return lists.reshape(GROUPS, KEYS, 2, PAIRS).astype(jnp.int32)


def draw_pair_count(key, part):
    base = jax.random.fold_in(key, 19)
    total = GROUPS * KEYS
    draws = jax.random.randint(base, (total,), 0, 1024, jnp.int32)
    counts = TC_DEV + (PAIRS - TC_DEV) * draws * draws // (1023 * 1023)
    busiest = jax.random.randint(jax.random.fold_in(base, 3), (), 0, total, jnp.int32)
    counts = counts.at[busiest].set(PAIRS)
    counts = counts.at[(busiest + 1) % total].set(TC_DEV)
    return counts.reshape(GROUPS, KEYS).astype(jnp.int32)


def block_levels(key, dims, pieces, least, top_value):
    gain = 1.0
    for dim, shards_of in pieces:
        steps = jax.random.uniform(jax.random.fold_in(jax.random.fold_in(key, 6), dim), (shards_of,), jnp.float32, least / len(pieces), top_value / len(pieces))
        gain = gain * jnp.repeat(jnp.exp(steps), dims[dim] // shards_of).reshape((-1,) + (1,) * (len(dims) - 1 - dim))
    return gain


def gaussian(stream_key, shape, spread, most, cuts=(), kind=jnp.bfloat16):
    level = block_levels(stream_key, shape, cuts, -0.22, 0.18) if cuts else 1.0
    array = jax.random.normal(stream_key, shape, jnp.float32) * spread * level
    return jnp.minimum(jnp.maximum(array, -most), most).astype(kind)


def setup_inputs(seed: int = 0) -> dict:
    keys = jax.random.split(jax.random.key(seed), 8)
    src_desc = draw_src_desc(jax.random.fold_in(keys[7], 71), 0)
    tgt_desc = draw_tgt_desc(jax.random.fold_in(keys[7], 71), 0)
    src_weight = jnp.clip(jnp.exp(math.log(20.0) - 5.9914645 * jax.random.uniform(keys[2], (NS,), jnp.float32) ** block_levels(keys[2], (NS,), ((0, 256),), -0.2, 0.2)), 0.05, 20.0)
    tgt_weight = jnp.clip(jnp.exp(math.log(20.0) - 5.9914645 * jax.random.uniform(keys[3], (NT,), jnp.float32) ** block_levels(keys[3], (NT,), ((0, 64),), -0.2, 0.2)), 0.05, 20.0)
    tgt_dual = gaussian(keys[4], (NT,), 0.2, 1.2, ((0, 64),), jnp.float32)
    pair_blocks = draw_pair_blocks(jax.random.fold_in(keys[7], 71), 0)
    pair_count = draw_pair_count(jax.random.fold_in(keys[7], 71), 0)
    return dict(src_desc=src_desc, tgt_desc=tgt_desc, src_weight=src_weight, tgt_weight=tgt_weight, tgt_dual=tgt_dual, pair_blocks=pair_blocks, pair_count=pair_count)


ENTROPY = 0.05


def reference(src_desc, tgt_desc, src_weight, tgt_weight, tgt_dual, pair_blocks, pair_count):
    sq_src = jnp.sum(src_desc.astype(jnp.float32) ** 2, axis=1) / DESC
    sq_tgt = jnp.sum(tgt_desc.astype(jnp.float32) ** 2, axis=1) / DESC
    devices_all = GROUPS * KEYS
    blocks = pair_blocks.reshape(devices_all, 2, PAIRS)
    counts = pair_count.reshape(devices_all)
    device_ids = jnp.arange(devices_all, dtype=jnp.int32)
    group_ids = device_ids // KEYS
    key_ids = device_ids % KEYS
    src_glob = (group_ids[:, None] * SG + blocks[:, 0, :]).reshape(-1).astype(jnp.int32)
    tgt_glob = (key_ids[:, None] * TC_DEV + blocks[:, 1, :]).reshape(-1).astype(jnp.int32)
    live = (jnp.arange(PAIRS, dtype=jnp.int32)[None, :] < counts[:, None]).reshape(-1)

    def block_cost(src_id, tgt_id):
        src_rows = lax.dynamic_slice_in_dim(src_desc, src_id * CLUSTER, CLUSTER, 0)
        tgt_rows = lax.dynamic_slice_in_dim(tgt_desc, tgt_id * CLUSTER, CLUSTER, 0)
        inner = lax.dot_general(src_rows, tgt_rows, (((1,), (1,)), ((), ())), preferred_element_type=jnp.float32)
        src_sq = lax.dynamic_slice_in_dim(sq_src, src_id * CLUSTER, CLUSTER, 0)
        tgt_sq = lax.dynamic_slice_in_dim(sq_tgt, tgt_id * CLUSTER, CLUSTER, 0)
        return src_sq[:, None] + tgt_sq[None, :] - (2.0 / DESC) * inner

    def first_sweep(carry, item):
        src_id, tgt_id, alive = item
        cost = block_cost(src_id, tgt_id)
        tgt_pot = lax.dynamic_slice_in_dim(tgt_dual, tgt_id * CLUSTER, CLUSTER, 0)
        rows_lse = jax.nn.logsumexp((tgt_pot[None, :] - cost) / ENTROPY, axis=1)
        rows_lse = jnp.where(alive, rows_lse, jnp.float32(-jnp.inf))
        old = lax.dynamic_index_in_dim(carry, src_id, 0, keepdims=False)
        return lax.dynamic_update_index_in_dim(carry, jnp.logaddexp(old, rows_lse), src_id, 0), None

    lse_src = jnp.full((NS // CLUSTER, CLUSTER), -jnp.inf, jnp.float32)
    lse_src, _ = lax.scan(first_sweep, lse_src, (src_glob, tgt_glob, live))
    src_dual = ENTROPY * jnp.log(src_weight) - ENTROPY * lse_src.reshape(-1)

    def second_sweep(carry, item):
        src_id, tgt_id, alive = item
        cost = block_cost(src_id, tgt_id)
        src_pot = lax.dynamic_slice_in_dim(src_dual, src_id * CLUSTER, CLUSTER, 0)
        cols_lse = jax.nn.logsumexp((src_pot[:, None] - cost) / ENTROPY, axis=0)
        cols_lse = jnp.where(alive, cols_lse, jnp.float32(-jnp.inf))
        old = lax.dynamic_index_in_dim(carry, tgt_id, 0, keepdims=False)
        return lax.dynamic_update_index_in_dim(carry, jnp.logaddexp(old, cols_lse), tgt_id, 0), None

    lse_tgt = jnp.full((NT // CLUSTER, CLUSTER), -jnp.inf, jnp.float32)
    lse_tgt, _ = lax.scan(second_sweep, lse_tgt, (src_glob, tgt_glob, live))
    tgt_dual_new = ENTROPY * jnp.log(tgt_weight) - ENTROPY * lse_tgt.reshape(-1)
    return (src_dual, tgt_dual_new)
```

```python
import functools

import jax
import jax.numpy as jnp
from jax import lax
from jax.experimental import pallas as pl
from jax.experimental.pallas import tpu as pltpu
from jax.sharding import PartitionSpec as P

CLUSTER = 256

ENTROPY = 0.05
INV_ENTROPY = 20.0
NEG_FLOOR = -1e30


def _slot_ids(ids_ref, slot, src_clusters, tgt_clusters):
    src_id = jnp.minimum(jnp.maximum(ids_ref[0, slot], 0), src_clusters - 1)
    tgt_id = jnp.minimum(jnp.maximum(ids_ref[1, slot], 0), tgt_clusters - 1)
    return src_id, tgt_id


def _block_cost(src_ref, tgt_ref, sqs_ref, sqt_ref, src_id, tgt_id, width):
    src_start = pl.multiple_of(src_id * CLUSTER, CLUSTER)
    tgt_start = pl.multiple_of(tgt_id * CLUSTER, CLUSTER)
    src_rows = src_ref[pl.ds(src_start, CLUSTER), :]
    tgt_rows = tgt_ref[pl.ds(tgt_start, CLUSTER), :]
    inner = lax.dot_general(
        tgt_rows, src_rows, (((1,), (1,)), ((), ())), preferred_element_type=jnp.float32
    )
    sq_s = sqs_ref[pl.ds(src_id, 1), :]
    sq_t = sqt_ref[pl.ds(tgt_start, CLUSTER), :]
    return (sq_s + sq_t) - (2.0 / width) * inner


def _first_kernel(ids_ref, cnt_ref, src_ref, tgt_ref, sqs_ref, sqt_ref, pot_ref, top_ref, tot_ref):
    src_clusters = sqs_ref.shape[0]
    tgt_clusters = tgt_ref.shape[0] // CLUSTER
    width = src_ref.shape[1]
    top_ref[...] = jnp.full(top_ref.shape, NEG_FLOOR, jnp.float32)
    tot_ref[...] = jnp.zeros(tot_ref.shape, jnp.float32)
    count = jnp.minimum(jnp.maximum(cnt_ref[0], 0), ids_ref.shape[1])

    def body(slot, carry):
        src_id, tgt_id = _slot_ids(ids_ref, slot, src_clusters, tgt_clusters)
        cost = _block_cost(src_ref, tgt_ref, sqs_ref, sqt_ref, src_id, tgt_id, width)
        pot = pot_ref[pl.ds(pl.multiple_of(tgt_id * CLUSTER, CLUSTER), CLUSTER), :]
        scores = (pot - cost) * INV_ENTROPY
        peak = jnp.max(scores, axis=0, keepdims=True)
        old_top = top_ref[pl.ds(src_id, 1), :]
        old_tot = tot_ref[pl.ds(src_id, 1), :]
        new_top = jnp.maximum(old_top, peak)
        new_tot = old_tot * jnp.exp(old_top - new_top) + jnp.sum(
            jnp.exp(scores - new_top), axis=0, keepdims=True
        )
        top_ref[pl.ds(src_id, 1), :] = new_top
        tot_ref[pl.ds(src_id, 1), :] = new_tot
        return carry

    lax.fori_loop(0, count, body, 0)


def _second_kernel(ids_ref, cnt_ref, src_ref, tgt_ref, sqs_ref, sqt_ref, dual_ref, top_ref, tot_ref):
    src_clusters = sqs_ref.shape[0]
    tgt_clusters = tgt_ref.shape[0] // CLUSTER
    width = src_ref.shape[1]
    top_ref[...] = jnp.full(top_ref.shape, NEG_FLOOR, jnp.float32)
    tot_ref[...] = jnp.zeros(tot_ref.shape, jnp.float32)
    count = jnp.minimum(jnp.maximum(cnt_ref[0], 0), ids_ref.shape[1])

    def body(slot, carry):
        src_id, tgt_id = _slot_ids(ids_ref, slot, src_clusters, tgt_clusters)
        cost = _block_cost(src_ref, tgt_ref, sqs_ref, sqt_ref, src_id, tgt_id, width)
        pot = dual_ref[pl.ds(src_id, 1), :]
        scores = (pot - cost) * INV_ENTROPY
        peak = jnp.max(scores, axis=1, keepdims=True)
        tgt_rows = pl.ds(pl.multiple_of(tgt_id * CLUSTER, CLUSTER), CLUSTER)
        old_top = top_ref[tgt_rows, :]
        old_tot = tot_ref[tgt_rows, :]
        new_top = jnp.maximum(old_top, peak)
        new_tot = old_tot * jnp.exp(old_top - new_top) + jnp.sum(
            jnp.exp(scores - new_top), axis=1, keepdims=True
        )
        top_ref[tgt_rows, :] = new_top
        tot_ref[tgt_rows, :] = new_tot
        return carry

    lax.fori_loop(0, count, body, 0)


def _sweep(kernel, out_shape, ids, cnt, group_src, tgt_desc, sq_src, sq_tgt, pot):
    vmem = pl.BlockSpec(memory_space=pltpu.VMEM)
    smem = pl.BlockSpec(memory_space=pltpu.SMEM)
    slots = ids.shape[1]
    flops = 2 * slots * CLUSTER * CLUSTER * group_src.shape[1]
    return pl.pallas_call(
        kernel,
        out_shape=(out_shape, out_shape),
        in_specs=[smem, smem, vmem, vmem, vmem, vmem, vmem],
        out_specs=(vmem, vmem),
        compiler_params=pltpu.CompilerParams(vmem_limit_bytes=48 * 1024 * 1024),
        cost_estimate=pl.CostEstimate(
            flops=flops,
            transcendentals=slots * CLUSTER * CLUSTER,
            bytes_accessed=group_src.size * 2 + tgt_desc.size * 2,
        ),
    )(ids, cnt, group_src, tgt_desc, sq_src, sq_tgt, pot)


def local(src_desc, tgt_desc, src_weight, tgt_weight, tgt_dual, pair_blocks, pair_count):
    width = src_desc.shape[1]
    own_clusters = src_desc.shape[0] // CLUSTER
    key_size = lax.axis_size("key")
    src_clusters = own_clusters * key_size
    tgt_clusters = tgt_desc.shape[0] // CLUSTER
    slot_total = pair_blocks.shape[3]
    ids = pair_blocks.reshape(2, slot_total)
    cnt = pair_count.reshape(1)

    sq_own = jnp.sum(src_desc.astype(jnp.float32) ** 2, axis=1) / width
    packed = jnp.stack([sq_own, src_weight]).reshape(2, own_clusters, CLUSTER)
    gathered = lax.all_gather(packed, "key", axis=1, tiled=True)
    sq_src = gathered[0]
    group_weight = gathered[1]
    group_src = lax.all_gather(src_desc, "key", axis=0, tiled=True)

    sq_tgt = (jnp.sum(tgt_desc.astype(jnp.float32) ** 2, axis=1) / width).reshape(-1, 1)
    pot_col = tgt_dual.reshape(-1, 1)

    src_shape = jax.ShapeDtypeStruct((src_clusters, CLUSTER), jnp.float32)
    src_tops, src_totals = _sweep(
        _first_kernel, src_shape, ids, cnt, group_src, tgt_desc, sq_src, sq_tgt, pot_col
    )
    full_top = lax.pmax(src_tops, "key")
    full_total = lax.psum(src_totals * jnp.exp(src_tops - full_top), "key")
    group_lse = full_top + jnp.log(full_total)
    group_dual = ENTROPY * jnp.log(group_weight) - ENTROPY * group_lse
    share_start = lax.axis_index("key") * own_clusters
    src_dual = lax.dynamic_slice_in_dim(group_dual, share_start, own_clusters, 0).reshape(-1)

    tgt_shape = jax.ShapeDtypeStruct((tgt_clusters * CLUSTER, 1), jnp.float32)
    tgt_tops, tgt_totals = _sweep(
        _second_kernel, tgt_shape, ids, cnt, group_src, tgt_desc, sq_src, sq_tgt, group_dual
    )
    tgt_pack = jnp.stack([tgt_tops.reshape(tgt_clusters, CLUSTER), tgt_totals.reshape(tgt_clusters, CLUSTER)])
    all_pack = lax.all_gather(tgt_pack, "group", axis=0)
    tops4 = all_pack[:, 0]
    tots4 = all_pack[:, 1]
    merged_top = jnp.max(tops4, axis=0)
    merged_total = jnp.sum(tots4 * jnp.exp(tops4 - merged_top[None]), axis=0)
    tgt_lse = (merged_top + jnp.log(merged_total)).reshape(-1)
    tgt_dual_new = ENTROPY * jnp.log(tgt_weight) - ENTROPY * tgt_lse
    return (src_dual, tgt_dual_new)


def solution(mesh):
    in_specs = (
        P(("group", "key"), None),
        P("key", None),
        P(("group", "key")),
        P("key"),
        P("key"),
        P("group", "key", None, None),
        P("group", "key"),
    )
    out_specs = (P(("group", "key")), P("key"))
    return jax.shard_map(local, mesh=mesh, in_specs=in_specs, out_specs=out_specs, check_vma=False)
```

```python
import functools

import jax
import jax.numpy as jnp
from jax import lax
from jax.experimental import pallas as pl
from jax.experimental.pallas import tpu as pltpu
from jax.sharding import PartitionSpec as P

CLUSTER = 256

ENTROPY = 0.05
INV_ENTROPY = 20.0
NEG_FLOOR = -1e30


def _slot_ids(ids_ref, slot, src_clusters, tgt_clusters):
    src_id = jnp.minimum(jnp.maximum(ids_ref[0, slot], 0), src_clusters - 1)
    tgt_id = jnp.minimum(jnp.maximum(ids_ref[1, slot], 0), tgt_clusters - 1)
    return src_id, tgt_id


def _block_cost(src_ref, tgt_ref, sqs_ref, sqt_ref, src_id, tgt_id, width):
    src_start = pl.multiple_of(src_id * CLUSTER, CLUSTER)
    tgt_start = pl.multiple_of(tgt_id * CLUSTER, CLUSTER)
    src_rows = src_ref[pl.ds(src_start, CLUSTER), :]
    tgt_rows = tgt_ref[pl.ds(tgt_start, CLUSTER), :]
    inner = lax.dot_general(
        tgt_rows, src_rows, (((1,), (1,)), ((), ())), preferred_element_type=jnp.float32
    )
    sq_s = sqs_ref[pl.ds(src_id, 1), :]
    sq_t = sqt_ref[pl.ds(tgt_start, CLUSTER), :]
    return (sq_s + sq_t) - (2.0 / width) * inner


def _first_kernel(ids_ref, cnt_ref, src_ref, tgt_ref, sqs_ref, sqt_ref, pot_ref, top_ref, tot_ref):
    src_clusters = sqs_ref.shape[0]
    tgt_clusters = tgt_ref.shape[0] // CLUSTER
    width = src_ref.shape[1]
    top_ref[...] = jnp.full(top_ref.shape, NEG_FLOOR, jnp.float32)
    tot_ref[...] = jnp.zeros(tot_ref.shape, jnp.float32)
    count = jnp.minimum(jnp.maximum(cnt_ref[0], 0), ids_ref.shape[1])

    def body(slot, carry):
        src_id, tgt_id = _slot_ids(ids_ref, slot, src_clusters, tgt_clusters)
        cost = _block_cost(src_ref, tgt_ref, sqs_ref, sqt_ref, src_id, tgt_id, width)
        pot = pot_ref[pl.ds(pl.multiple_of(tgt_id * CLUSTER, CLUSTER), CLUSTER), :]
        scores = (pot - cost) * INV_ENTROPY
        peak = jnp.max(scores, axis=0, keepdims=True)
        old_top = top_ref[pl.ds(src_id, 1), :]
        old_tot = tot_ref[pl.ds(src_id, 1), :]
        new_top = jnp.maximum(old_top, peak)
        new_tot = old_tot * jnp.exp(old_top - new_top) + jnp.sum(
            jnp.exp(scores - new_top), axis=0, keepdims=True
        )
        top_ref[pl.ds(src_id, 1), :] = new_top
        tot_ref[pl.ds(src_id, 1), :] = new_tot
        return carry

    lax.fori_loop(0, count, body, 0)


def _second_kernel(ids_ref, cnt_ref, src_ref, tgt_ref, sqs_ref, sqt_ref, dual_ref, top_ref, tot_ref):
    src_clusters = sqs_ref.shape[0]
    tgt_clusters = tgt_ref.shape[0] // CLUSTER
    width = src_ref.shape[1]
    top_ref[...] = jnp.full(top_ref.shape, NEG_FLOOR, jnp.float32)
    tot_ref[...] = jnp.zeros(tot_ref.shape, jnp.float32)
    count = jnp.minimum(jnp.maximum(cnt_ref[0], 0), ids_ref.shape[1])

    def body(slot, carry):
        src_id, tgt_id = _slot_ids(ids_ref, slot, src_clusters, tgt_clusters)
        cost = _block_cost(src_ref, tgt_ref, sqs_ref, sqt_ref, src_id, tgt_id, width)
        pot = dual_ref[pl.ds(src_id, 1), :]
        scores = (pot - cost) * INV_ENTROPY
        peak = jnp.max(scores, axis=1, keepdims=True)
        tgt_rows = pl.ds(pl.multiple_of(tgt_id * CLUSTER, CLUSTER), CLUSTER)
        old_top = top_ref[tgt_rows, :]
        old_tot = tot_ref[tgt_rows, :]
        new_top = jnp.maximum(old_top, peak)
        new_tot = old_tot * jnp.exp(old_top - new_top) + jnp.sum(
            jnp.exp(scores - new_top), axis=1, keepdims=True
        )
        top_ref[tgt_rows, :] = new_top
        tot_ref[tgt_rows, :] = new_tot
        return carry

    lax.fori_loop(0, count, body, 0)


def _sweep(kernel, out_shape, ids, cnt, group_src, tgt_desc, sq_src, sq_tgt, pot):
    vmem = pl.BlockSpec(memory_space=pltpu.VMEM)
    smem = pl.BlockSpec(memory_space=pltpu.SMEM)
    slots = ids.shape[1]
    flops = 2 * slots * CLUSTER * CLUSTER * group_src.shape[1]
    return pl.pallas_call(
        kernel,
        out_shape=(out_shape, out_shape),
        in_specs=[smem, smem, vmem, vmem, vmem, vmem, vmem],
        out_specs=(vmem, vmem),
        compiler_params=pltpu.CompilerParams(vmem_limit_bytes=48 * 1024 * 1024),
        cost_estimate=pl.CostEstimate(
            flops=flops,
            transcendentals=slots * CLUSTER * CLUSTER,
            bytes_accessed=group_src.size * 2 + tgt_desc.size * 2,
        ),
    )(ids, cnt, group_src, tgt_desc, sq_src, sq_tgt, pot)


def merge(low, high):
    top = jnp.maximum(low[0], high[0])
    total = low[1] * jnp.exp(low[0] - top) + high[1] * jnp.exp(high[0] - top)
    return jnp.concatenate([top[None], total[None], low[2:] + high[2:]], axis=0)


def butterfly(planes, axis, size, index):
    bit = 1
    while bit < size:
        perm = [(i, i ^ bit) for i in range(size)]
        other = lax.ppermute(planes, axis, perm)
        is_low = (index & bit) == 0
        low = jnp.where(is_low, planes, other)
        high = jnp.where(is_low, other, planes)
        planes = merge(low, high)
        bit *= 2
    return planes


def local(src_desc, tgt_desc, src_weight, tgt_weight, tgt_dual, pair_blocks, pair_count):
    width = src_desc.shape[1]
    own_clusters = src_desc.shape[0] // CLUSTER
    key_size = lax.axis_size("key")
    src_clusters = own_clusters * key_size
    tgt_clusters = tgt_desc.shape[0] // CLUSTER
    slot_total = pair_blocks.shape[3]
    ids = pair_blocks.reshape(2, slot_total)
    cnt = pair_count.reshape(1)

    group_src = lax.all_gather(src_desc, "key", axis=0, tiled=True)
    sq_src = (jnp.sum(group_src.astype(jnp.float32) ** 2, axis=1) / width).reshape(src_clusters, CLUSTER)

    sq_tgt = (jnp.sum(tgt_desc.astype(jnp.float32) ** 2, axis=1) / width).reshape(-1, 1)
    pot_col = tgt_dual.reshape(-1, 1)

    src_shape = jax.ShapeDtypeStruct((src_clusters, CLUSTER), jnp.float32)
    src_tops, src_totals = _sweep(
        _first_kernel, src_shape, ids, cnt, group_src, tgt_desc, sq_src, sq_tgt, pot_col
    )
    key_index = lax.axis_index("key")
    own_rows = lax.broadcasted_iota(jnp.int32, (src_clusters, CLUSTER), 0) // own_clusters == key_index
    own_weight = jnp.tile(src_weight.reshape(own_clusters, CLUSTER), (key_size, 1))
    weight_rows = jnp.where(own_rows, own_weight, jnp.zeros_like(own_weight))
    full_top, full_total, group_weight = butterfly(
        jnp.stack([src_tops, src_totals, weight_rows]), "key", key_size, key_index
    )
    group_lse = full_top + jnp.log(full_total)
    group_dual = ENTROPY * jnp.log(group_weight) - ENTROPY * group_lse
    share_start = key_index * own_clusters
    src_dual = lax.dynamic_slice_in_dim(group_dual, share_start, own_clusters, 0).reshape(-1)

    tgt_shape = jax.ShapeDtypeStruct((tgt_clusters * CLUSTER, 1), jnp.float32)
    tgt_tops, tgt_totals = _sweep(
        _second_kernel, tgt_shape, ids, cnt, group_src, tgt_desc, sq_src, sq_tgt, group_dual
    )
    tgt_pack = jnp.stack([tgt_tops.reshape(tgt_clusters, CLUSTER), tgt_totals.reshape(tgt_clusters, CLUSTER)])
    all_pack = lax.all_gather(tgt_pack, "group", axis=0)
    tops4 = all_pack[:, 0]
    tots4 = all_pack[:, 1]
    merged_top = jnp.max(tops4, axis=0)
    merged_total = jnp.sum(tots4 * jnp.exp(tops4 - merged_top[None]), axis=0)
    tgt_lse = (merged_top + jnp.log(merged_total)).reshape(-1)
    tgt_dual_new = ENTROPY * jnp.log(tgt_weight) - ENTROPY * tgt_lse
    return (src_dual, tgt_dual_new)


def solution(mesh):
    in_specs = (
        P(("group", "key"), None),
        P("key", None),
        P(("group", "key")),
        P("key"),
        P("key"),
        P("group", "key", None, None),
        P("group", "key"),
    )
    out_specs = (P(("group", "key")), P("key"))
    return jax.shard_map(local, mesh=mesh, in_specs=in_specs, out_specs=out_specs, check_vma=False)
```

```python
import functools

import jax
import jax.numpy as jnp
from jax import lax
from jax.experimental import pallas as pl
from jax.experimental.pallas import tpu as pltpu
from jax.sharding import PartitionSpec as P

CLUSTER = 256
CORES = 2

ENTROPY = 0.05
INV_ENTROPY = 20.0
NEG_FLOOR = -1e30
KEY = ("chip", "core")


def _slot_ids(ids_ref, slot, src_clusters, tgt_clusters):
    src_id = jnp.minimum(jnp.maximum(ids_ref[0, slot], 0), src_clusters - 1)
    tgt_id = jnp.minimum(jnp.maximum(ids_ref[1, slot], 0), tgt_clusters - 1)
    return src_id, tgt_id


def _src_position(src_id, src_clusters):
    return (src_id % CORES) * (src_clusters // CORES) + src_id // CORES


def _block_cost(src_ref, tgt_ref, sqs_ref, sqt_ref, src_id, tgt_id, width):
    src_pos = _src_position(src_id, sqs_ref.shape[0])
    src_start = pl.multiple_of(src_pos * CLUSTER, CLUSTER)
    tgt_start = pl.multiple_of(tgt_id * CLUSTER, CLUSTER)
    src_rows = src_ref[pl.ds(src_start, CLUSTER), :]
    tgt_rows = tgt_ref[pl.ds(tgt_start, CLUSTER), :]
    inner = lax.dot_general(
        tgt_rows, src_rows, (((1,), (1,)), ((), ())), preferred_element_type=jnp.float32
    )
    sq_s = sqs_ref[pl.ds(src_pos, 1), :]
    sq_t = sqt_ref[pl.ds(tgt_start, CLUSTER), :]
    return (sq_s + sq_t) - (2.0 / width) * inner


def _first_kernel(ids_ref, cnt_ref, src_ref, tgt_ref, sqs_ref, sqt_ref, pot_ref, top_ref, tot_ref):
    src_clusters = sqs_ref.shape[0]
    tgt_clusters = tgt_ref.shape[0] // CLUSTER
    width = src_ref.shape[1]
    top_ref[...] = jnp.full(top_ref.shape, NEG_FLOOR, jnp.float32)
    tot_ref[...] = jnp.zeros(tot_ref.shape, jnp.float32)
    count = jnp.minimum(jnp.maximum(cnt_ref[0], 0), ids_ref.shape[1])

    def body(slot, carry):
        src_id, tgt_id = _slot_ids(ids_ref, slot, src_clusters, tgt_clusters)
        cost = _block_cost(src_ref, tgt_ref, sqs_ref, sqt_ref, src_id, tgt_id, width)
        pot = pot_ref[pl.ds(pl.multiple_of(tgt_id * CLUSTER, CLUSTER), CLUSTER), :]
        scores = (pot - cost) * INV_ENTROPY
        peak = jnp.max(scores, axis=0, keepdims=True)
        old_top = top_ref[pl.ds(src_id, 1), :]
        old_tot = tot_ref[pl.ds(src_id, 1), :]
        new_top = jnp.maximum(old_top, peak)
        new_tot = old_tot * jnp.exp(old_top - new_top) + jnp.sum(
            jnp.exp(scores - new_top), axis=0, keepdims=True
        )
        top_ref[pl.ds(src_id, 1), :] = new_top
        tot_ref[pl.ds(src_id, 1), :] = new_tot
        return carry

    lax.fori_loop(0, count, body, 0)


def _second_kernel(ids_ref, cnt_ref, src_ref, tgt_ref, sqs_ref, sqt_ref, dual_ref, top_ref, tot_ref):
    src_clusters = sqs_ref.shape[0]
    tgt_clusters = tgt_ref.shape[0] // CLUSTER
    width = src_ref.shape[1]
    top_ref[...] = jnp.full(top_ref.shape, NEG_FLOOR, jnp.float32)
    tot_ref[...] = jnp.zeros(tot_ref.shape, jnp.float32)
    count = jnp.minimum(jnp.maximum(cnt_ref[0], 0), ids_ref.shape[1])

    def body(slot, carry):
        src_id, tgt_id = _slot_ids(ids_ref, slot, src_clusters, tgt_clusters)
        cost = _block_cost(src_ref, tgt_ref, sqs_ref, sqt_ref, src_id, tgt_id, width)
        pot = dual_ref[pl.ds(src_id, 1), :]
        scores = (pot - cost) * INV_ENTROPY
        peak = jnp.max(scores, axis=1, keepdims=True)
        tgt_rows = pl.ds(pl.multiple_of(tgt_id * CLUSTER, CLUSTER), CLUSTER)
        old_top = top_ref[tgt_rows, :]
        old_tot = tot_ref[tgt_rows, :]
        new_top = jnp.maximum(old_top, peak)
        new_tot = old_tot * jnp.exp(old_top - new_top) + jnp.sum(
            jnp.exp(scores - new_top), axis=1, keepdims=True
        )
        top_ref[tgt_rows, :] = new_top
        tot_ref[tgt_rows, :] = new_tot
        return carry

    lax.fori_loop(0, count, body, 0)


def _sweep(kernel, out_shape, ids, cnt, group_src, tgt_desc, sq_src, sq_tgt, pot):
    vmem = pl.BlockSpec(memory_space=pltpu.VMEM)
    smem = pl.BlockSpec(memory_space=pltpu.SMEM)
    slots = ids.shape[1]
    flops = 2 * slots * CLUSTER * CLUSTER * group_src.shape[1]
    return pl.pallas_call(
        kernel,
        out_shape=(out_shape, out_shape),
        in_specs=[smem, smem, vmem, vmem, vmem, vmem, vmem],
        out_specs=(vmem, vmem),
        compiler_params=pltpu.CompilerParams(vmem_limit_bytes=48 * 1024 * 1024),
        cost_estimate=pl.CostEstimate(
            flops=flops,
            transcendentals=slots * CLUSTER * CLUSTER,
            bytes_accessed=group_src.size * 2 + tgt_desc.size * 2,
        ),
    )(ids, cnt, group_src, tgt_desc, sq_src, sq_tgt, pot)


def merge(low, high):
    top = jnp.maximum(low[0], high[0])
    total = low[1] * jnp.exp(low[0] - top) + high[1] * jnp.exp(high[0] - top)
    return jnp.concatenate([top[None], total[None], low[2:] + high[2:]], axis=0)


def butterfly(planes, axis, size, index):
    bit = 1
    while bit < size:
        perm = [(i, i ^ bit) for i in range(size)]
        other = lax.ppermute(planes, axis, perm)
        is_low = (index & bit) == 0
        low = jnp.where(is_low, planes, other)
        high = jnp.where(is_low, other, planes)
        planes = merge(low, high)
        bit *= 2
    return planes


def local(src_desc, tgt_desc, src_weight, tgt_weight, tgt_dual, pair_blocks, pair_count):
    width = src_desc.shape[1]
    own_clusters = src_desc.shape[0] // CLUSTER
    key_size = lax.axis_size(KEY)
    src_clusters = own_clusters * key_size
    tgt_clusters = tgt_desc.shape[0] // CLUSTER
    slot_total = pair_blocks.shape[3]
    ids = pair_blocks.reshape(2, slot_total)
    cnt = pair_count.reshape(1)

    chip_src = lax.all_gather(src_desc, "chip", axis=0, tiled=True)
    group_src = lax.all_gather(chip_src, "core", axis=0, tiled=True)
    sq_src = (jnp.sum(group_src.astype(jnp.float32) ** 2, axis=1) / width).reshape(src_clusters, CLUSTER)

    sq_tgt = (jnp.sum(tgt_desc.astype(jnp.float32) ** 2, axis=1) / width).reshape(-1, 1)
    pot_col = tgt_dual.reshape(-1, 1)

    src_shape = jax.ShapeDtypeStruct((src_clusters, CLUSTER), jnp.float32)
    src_tops, src_totals = _sweep(
        _first_kernel, src_shape, ids, cnt, group_src, tgt_desc, sq_src, sq_tgt, pot_col
    )
    key_index = lax.axis_index(KEY)
    own_rows = lax.broadcasted_iota(jnp.int32, (src_clusters, CLUSTER), 0) // own_clusters == key_index
    own_weight = jnp.tile(src_weight.reshape(own_clusters, CLUSTER), (key_size, 1))
    weight_rows = jnp.where(own_rows, own_weight, jnp.zeros_like(own_weight))
    full_top, full_total, group_weight = butterfly(
        jnp.stack([src_tops, src_totals, weight_rows]), KEY, key_size, key_index
    )
    group_lse = full_top + jnp.log(full_total)
    group_dual = ENTROPY * jnp.log(group_weight) - ENTROPY * group_lse
    share_start = key_index * own_clusters
    src_dual = lax.dynamic_slice_in_dim(group_dual, share_start, own_clusters, 0).reshape(-1)

    tgt_shape = jax.ShapeDtypeStruct((tgt_clusters * CLUSTER, 1), jnp.float32)
    tgt_tops, tgt_totals = _sweep(
        _second_kernel, tgt_shape, ids, cnt, group_src, tgt_desc, sq_src, sq_tgt, group_dual
    )
    tgt_pack = jnp.stack([tgt_tops.reshape(tgt_clusters, CLUSTER), tgt_totals.reshape(tgt_clusters, CLUSTER)])
    all_pack = lax.all_gather(tgt_pack, "group", axis=0)
    tops4 = all_pack[:, 0]
    tots4 = all_pack[:, 1]
    merged_top = jnp.max(tops4, axis=0)
    merged_total = jnp.sum(tots4 * jnp.exp(tops4 - merged_top[None]), axis=0)
    tgt_lse = (merged_top + jnp.log(merged_total)).reshape(-1)
    tgt_dual_new = ENTROPY * jnp.log(tgt_weight) - ENTROPY * tgt_lse
    return (src_dual, tgt_dual_new)


def solution(mesh):
    groups, keys = mesh.devices.shape
    split = jax.sharding.Mesh(mesh.devices.reshape(groups, keys // CORES, CORES), ("group",) + KEY)
    in_specs = (
        P(("group",) + KEY, None),
        P(KEY, None),
        P(("group",) + KEY),
        P(KEY),
        P(KEY),
        P("group", KEY, None, None),
        P("group", KEY),
    )
    out_specs = (P(("group",) + KEY), P(KEY))
    return jax.shard_map(local, mesh=split, in_specs=in_specs, out_specs=out_specs, check_vma=False)
```

```python
import functools

import jax
import jax.numpy as jnp
from jax import lax
from jax.experimental import pallas as pl
from jax.experimental.pallas import tpu as pltpu
from jax.sharding import PartitionSpec as P

CLUSTER = 256

ENTROPY = 0.05
INV_ENTROPY = 20.0
NEG_FLOOR = -1e30


def _slot_ids(ids_ref, slot, src_clusters, tgt_clusters):
    src_id = jnp.minimum(jnp.maximum(ids_ref[0, slot], 0), src_clusters - 1)
    tgt_id = jnp.minimum(jnp.maximum(ids_ref[1, slot], 0), tgt_clusters - 1)
    return src_id, tgt_id


def _block_cost(src_ref, tgt_ref, sqs_ref, sqt_ref, src_id, tgt_id, width):
    src_start = pl.multiple_of(src_id * CLUSTER, CLUSTER)
    tgt_start = pl.multiple_of(tgt_id * CLUSTER, CLUSTER)
    src_rows = src_ref[pl.ds(src_start, CLUSTER), :]
    tgt_rows = tgt_ref[pl.ds(tgt_start, CLUSTER), :]
    inner = lax.dot_general(
        tgt_rows, src_rows, (((1,), (1,)), ((), ())), preferred_element_type=jnp.float32
    )
    sq_s = sqs_ref[pl.ds(src_id, 1), :]
    sq_t = sqt_ref[pl.ds(tgt_start, CLUSTER), :]
    return (sq_s + sq_t) - (2.0 / width) * inner


def _first_kernel(ids_ref, cnt_ref, src_ref, tgt_ref, sqs_ref, sqt_ref, pot_ref, top_ref, tot_ref):
    src_clusters = sqs_ref.shape[0]
    tgt_clusters = tgt_ref.shape[0] // CLUSTER
    width = src_ref.shape[1]
    top_ref[...] = jnp.full(top_ref.shape, NEG_FLOOR, jnp.float32)
    tot_ref[...] = jnp.zeros(tot_ref.shape, jnp.float32)
    count = jnp.minimum(jnp.maximum(cnt_ref[0], 0), ids_ref.shape[1])

    def scores_of(slot):
        src_id, tgt_id = _slot_ids(ids_ref, slot, src_clusters, tgt_clusters)
        cost = _block_cost(src_ref, tgt_ref, sqs_ref, sqt_ref, src_id, tgt_id, width)
        pot = pot_ref[pl.ds(pl.multiple_of(tgt_id * CLUSTER, CLUSTER), CLUSTER), :]
        return src_id, (pot - cost) * INV_ENTROPY

    def update(src_id, scores):
        peak = jnp.max(scores, axis=0, keepdims=True)
        old_top = top_ref[pl.ds(src_id, 1), :]
        old_tot = tot_ref[pl.ds(src_id, 1), :]
        new_top = jnp.maximum(old_top, peak)
        new_tot = old_tot * jnp.exp(old_top - new_top) + jnp.sum(
            jnp.exp(scores - new_top), axis=0, keepdims=True
        )
        top_ref[pl.ds(src_id, 1), :] = new_top
        tot_ref[pl.ds(src_id, 1), :] = new_tot

    def body(trip, carry):
        first = scores_of(2 * trip)
        second = scores_of(2 * trip + 1)
        update(*first)
        update(*second)
        return carry

    lax.fori_loop(0, count // 2, body, 0)

    @pl.when(count % 2 == 1)
    def _():
        update(*scores_of(count - 1))


def _second_kernel(ids_ref, cnt_ref, src_ref, tgt_ref, sqs_ref, sqt_ref, dual_ref, top_ref, tot_ref):
    src_clusters = sqs_ref.shape[0]
    tgt_clusters = tgt_ref.shape[0] // CLUSTER
    width = src_ref.shape[1]
    top_ref[...] = jnp.full(top_ref.shape, NEG_FLOOR, jnp.float32)
    tot_ref[...] = jnp.zeros(tot_ref.shape, jnp.float32)
    count = jnp.minimum(jnp.maximum(cnt_ref[0], 0), ids_ref.shape[1])

    def scores_of(slot):
        src_id, tgt_id = _slot_ids(ids_ref, slot, src_clusters, tgt_clusters)
        cost = _block_cost(src_ref, tgt_ref, sqs_ref, sqt_ref, src_id, tgt_id, width)
        pot = dual_ref[pl.ds(src_id, 1), :]
        return tgt_id, (pot - cost) * INV_ENTROPY

    def update(tgt_id, scores):
        peak = jnp.max(scores, axis=1, keepdims=True)
        tgt_rows = pl.ds(pl.multiple_of(tgt_id * CLUSTER, CLUSTER), CLUSTER)
        old_top = top_ref[tgt_rows, :]
        old_tot = tot_ref[tgt_rows, :]
        new_top = jnp.maximum(old_top, peak)
        new_tot = old_tot * jnp.exp(old_top - new_top) + jnp.sum(
            jnp.exp(scores - new_top), axis=1, keepdims=True
        )
        top_ref[tgt_rows, :] = new_top
        tot_ref[tgt_rows, :] = new_tot

    def body(trip, carry):
        first = scores_of(2 * trip)
        second = scores_of(2 * trip + 1)
        update(*first)
        update(*second)
        return carry

    lax.fori_loop(0, count // 2, body, 0)

    @pl.when(count % 2 == 1)
    def _():
        update(*scores_of(count - 1))


def _sweep(kernel, out_shape, ids, cnt, group_src, tgt_desc, sq_src, sq_tgt, pot):
    vmem = pl.BlockSpec(memory_space=pltpu.VMEM)
    smem = pl.BlockSpec(memory_space=pltpu.SMEM)
    slots = ids.shape[1]
    flops = 2 * slots * CLUSTER * CLUSTER * group_src.shape[1]
    return pl.pallas_call(
        kernel,
        out_shape=(out_shape, out_shape),
        in_specs=[smem, smem, vmem, vmem, vmem, vmem, vmem],
        out_specs=(vmem, vmem),
        compiler_params=pltpu.CompilerParams(vmem_limit_bytes=48 * 1024 * 1024),
        cost_estimate=pl.CostEstimate(
            flops=flops,
            transcendentals=slots * CLUSTER * CLUSTER,
            bytes_accessed=group_src.size * 2 + tgt_desc.size * 2,
        ),
    )(ids, cnt, group_src, tgt_desc, sq_src, sq_tgt, pot)


def merge(low, high):
    top = jnp.maximum(low[0], high[0])
    total = low[1] * jnp.exp(low[0] - top) + high[1] * jnp.exp(high[0] - top)
    return jnp.concatenate([top[None], total[None], low[2:] + high[2:]], axis=0)


def butterfly(planes, axis, size, index):
    bit = 1
    while bit < size:
        perm = [(i, i ^ bit) for i in range(size)]
        other = lax.ppermute(planes, axis, perm)
        is_low = (index & bit) == 0
        low = jnp.where(is_low, planes, other)
        high = jnp.where(is_low, other, planes)
        planes = merge(low, high)
        bit *= 2
    return planes


def local(src_desc, tgt_desc, src_weight, tgt_weight, tgt_dual, pair_blocks, pair_count):
    width = src_desc.shape[1]
    own_clusters = src_desc.shape[0] // CLUSTER
    key_size = lax.axis_size("key")
    src_clusters = own_clusters * key_size
    tgt_clusters = tgt_desc.shape[0] // CLUSTER
    slot_total = pair_blocks.shape[3]
    ids = pair_blocks.reshape(2, slot_total)
    cnt = pair_count.reshape(1)

    group_src = lax.all_gather(src_desc, "key", axis=0, tiled=True)
    sq_src = (jnp.sum(group_src.astype(jnp.float32) ** 2, axis=1) / width).reshape(src_clusters, CLUSTER)

    sq_tgt = (jnp.sum(tgt_desc.astype(jnp.float32) ** 2, axis=1) / width).reshape(-1, 1)
    pot_col = tgt_dual.reshape(-1, 1)

    src_shape = jax.ShapeDtypeStruct((src_clusters, CLUSTER), jnp.float32)
    src_tops, src_totals = _sweep(
        _first_kernel, src_shape, ids, cnt, group_src, tgt_desc, sq_src, sq_tgt, pot_col
    )
    key_index = lax.axis_index("key")
    own_rows = lax.broadcasted_iota(jnp.int32, (src_clusters, CLUSTER), 0) // own_clusters == key_index
    own_weight = jnp.tile(src_weight.reshape(own_clusters, CLUSTER), (key_size, 1))
    weight_rows = jnp.where(own_rows, own_weight, jnp.zeros_like(own_weight))
    full_top, full_total, group_weight = butterfly(
        jnp.stack([src_tops, src_totals, weight_rows]), "key", key_size, key_index
    )
    group_lse = full_top + jnp.log(full_total)
    group_dual = ENTROPY * jnp.log(group_weight) - ENTROPY * group_lse
    share_start = key_index * own_clusters
    src_dual = lax.dynamic_slice_in_dim(group_dual, share_start, own_clusters, 0).reshape(-1)

    tgt_shape = jax.ShapeDtypeStruct((tgt_clusters * CLUSTER, 1), jnp.float32)
    tgt_tops, tgt_totals = _sweep(
        _second_kernel, tgt_shape, ids, cnt, group_src, tgt_desc, sq_src, sq_tgt, group_dual
    )
    tgt_pack = jnp.stack([tgt_tops.reshape(tgt_clusters, CLUSTER), tgt_totals.reshape(tgt_clusters, CLUSTER)])
    all_pack = lax.all_gather(tgt_pack, "group", axis=0)
    tops4 = all_pack[:, 0]
    tots4 = all_pack[:, 1]
    merged_top = jnp.max(tops4, axis=0)
    merged_total = jnp.sum(tots4 * jnp.exp(tops4 - merged_top[None]), axis=0)
    tgt_lse = (merged_top + jnp.log(merged_total)).reshape(-1)
    tgt_dual_new = ENTROPY * jnp.log(tgt_weight) - ENTROPY * tgt_lse
    return (src_dual, tgt_dual_new)


def solution(mesh):
    in_specs = (
        P(("group", "key"), None),
        P("key", None),
        P(("group", "key")),
        P("key"),
        P("key"),
        P("group", "key", None, None),
        P("group", "key"),
    )
    out_specs = (P(("group", "key")), P("key"))
    return jax.shard_map(local, mesh=mesh, in_specs=in_specs, out_specs=out_specs, check_vma=False)
```

```python
import functools

import jax
import jax.numpy as jnp
from jax import lax
from jax.experimental import pallas as pl
from jax.experimental.pallas import tpu as pltpu
from jax.sharding import PartitionSpec as P

CLUSTER = 256
UNROLL = 4

ENTROPY = 0.05
INV_ENTROPY = 20.0
NEG_FLOOR = -1e30


def _slot_ids(ids_ref, slot, src_clusters, tgt_clusters):
    src_id = jnp.minimum(jnp.maximum(ids_ref[0, slot], 0), src_clusters - 1)
    tgt_id = jnp.minimum(jnp.maximum(ids_ref[1, slot], 0), tgt_clusters - 1)
    return src_id, tgt_id


def _block_cost(src_ref, tgt_ref, sqs_ref, sqt_ref, src_id, tgt_id, width):
    src_start = pl.multiple_of(src_id * CLUSTER, CLUSTER)
    tgt_start = pl.multiple_of(tgt_id * CLUSTER, CLUSTER)
    src_rows = src_ref[pl.ds(src_start, CLUSTER), :]
    tgt_rows = tgt_ref[pl.ds(tgt_start, CLUSTER), :]
    inner = lax.dot_general(
        tgt_rows, src_rows, (((1,), (1,)), ((), ())), preferred_element_type=jnp.float32
    )
    sq_s = sqs_ref[pl.ds(src_id, 1), :]
    sq_t = sqt_ref[pl.ds(tgt_start, CLUSTER), :]
    return (sq_s + sq_t) - (2.0 / width) * inner


def _first_kernel(ids_ref, cnt_ref, src_ref, tgt_ref, sqs_ref, sqt_ref, pot_ref, top_ref, tot_ref):
    src_clusters = sqs_ref.shape[0]
    tgt_clusters = tgt_ref.shape[0] // CLUSTER
    width = src_ref.shape[1]
    top_ref[...] = jnp.full(top_ref.shape, NEG_FLOOR, jnp.float32)
    tot_ref[...] = jnp.zeros(tot_ref.shape, jnp.float32)
    count = jnp.minimum(jnp.maximum(cnt_ref[0], 0), ids_ref.shape[1])

    def scores_of(slot):
        src_id, tgt_id = _slot_ids(ids_ref, slot, src_clusters, tgt_clusters)
        cost = _block_cost(src_ref, tgt_ref, sqs_ref, sqt_ref, src_id, tgt_id, width)
        pot = pot_ref[pl.ds(pl.multiple_of(tgt_id * CLUSTER, CLUSTER), CLUSTER), :]
        return src_id, (pot - cost) * INV_ENTROPY

    def update(src_id, scores):
        peak = jnp.max(scores, axis=0, keepdims=True)
        old_top = top_ref[pl.ds(src_id, 1), :]
        old_tot = tot_ref[pl.ds(src_id, 1), :]
        new_top = jnp.maximum(old_top, peak)
        new_tot = old_tot * jnp.exp(old_top - new_top) + jnp.sum(
            jnp.exp(scores - new_top), axis=0, keepdims=True
        )
        top_ref[pl.ds(src_id, 1), :] = new_top
        tot_ref[pl.ds(src_id, 1), :] = new_tot

    def body(trip, carry):
        blocks = [scores_of(UNROLL * trip + lane) for lane in range(UNROLL)]
        for block in blocks:
            update(*block)
        return carry

    def tail(slot, carry):
        update(*scores_of(slot))
        return carry

    lax.fori_loop(0, count // UNROLL, body, 0)
    lax.fori_loop(count // UNROLL * UNROLL, count, tail, 0)


def _second_kernel(ids_ref, cnt_ref, src_ref, tgt_ref, sqs_ref, sqt_ref, dual_ref, top_ref, tot_ref):
    src_clusters = sqs_ref.shape[0]
    tgt_clusters = tgt_ref.shape[0] // CLUSTER
    width = src_ref.shape[1]
    top_ref[...] = jnp.full(top_ref.shape, NEG_FLOOR, jnp.float32)
    tot_ref[...] = jnp.zeros(tot_ref.shape, jnp.float32)
    count = jnp.minimum(jnp.maximum(cnt_ref[0], 0), ids_ref.shape[1])

    def scores_of(slot):
        src_id, tgt_id = _slot_ids(ids_ref, slot, src_clusters, tgt_clusters)
        cost = _block_cost(src_ref, tgt_ref, sqs_ref, sqt_ref, src_id, tgt_id, width)
        pot = dual_ref[pl.ds(src_id, 1), :]
        return tgt_id, (pot - cost) * INV_ENTROPY

    def update(tgt_id, scores):
        peak = jnp.max(scores, axis=1, keepdims=True)
        tgt_rows = pl.ds(pl.multiple_of(tgt_id * CLUSTER, CLUSTER), CLUSTER)
        old_top = top_ref[tgt_rows, :]
        old_tot = tot_ref[tgt_rows, :]
        new_top = jnp.maximum(old_top, peak)
        new_tot = old_tot * jnp.exp(old_top - new_top) + jnp.sum(
            jnp.exp(scores - new_top), axis=1, keepdims=True
        )
        top_ref[tgt_rows, :] = new_top
        tot_ref[tgt_rows, :] = new_tot

    def body(trip, carry):
        blocks = [scores_of(UNROLL * trip + lane) for lane in range(UNROLL)]
        for block in blocks:
            update(*block)
        return carry

    def tail(slot, carry):
        update(*scores_of(slot))
        return carry

    lax.fori_loop(0, count // UNROLL, body, 0)
    lax.fori_loop(count // UNROLL * UNROLL, count, tail, 0)


def _sweep(kernel, out_shape, ids, cnt, group_src, tgt_desc, sq_src, sq_tgt, pot):
    vmem = pl.BlockSpec(memory_space=pltpu.VMEM)
    smem = pl.BlockSpec(memory_space=pltpu.SMEM)
    slots = ids.shape[1]
    flops = 2 * slots * CLUSTER * CLUSTER * group_src.shape[1]
    return pl.pallas_call(
        kernel,
        out_shape=(out_shape, out_shape),
        in_specs=[smem, smem, vmem, vmem, vmem, vmem, vmem],
        out_specs=(vmem, vmem),
        compiler_params=pltpu.CompilerParams(vmem_limit_bytes=48 * 1024 * 1024),
        cost_estimate=pl.CostEstimate(
            flops=flops,
            transcendentals=slots * CLUSTER * CLUSTER,
            bytes_accessed=group_src.size * 2 + tgt_desc.size * 2,
        ),
    )(ids, cnt, group_src, tgt_desc, sq_src, sq_tgt, pot)


def merge(low, high):
    top = jnp.maximum(low[0], high[0])
    total = low[1] * jnp.exp(low[0] - top) + high[1] * jnp.exp(high[0] - top)
    return jnp.concatenate([top[None], total[None], low[2:] + high[2:]], axis=0)


def butterfly(planes, axis, size, index):
    bit = 1
    while bit < size:
        perm = [(i, i ^ bit) for i in range(size)]
        other = lax.ppermute(planes, axis, perm)
        is_low = (index & bit) == 0
        low = jnp.where(is_low, planes, other)
        high = jnp.where(is_low, other, planes)
        planes = merge(low, high)
        bit *= 2
    return planes


def local(src_desc, tgt_desc, src_weight, tgt_weight, tgt_dual, pair_blocks, pair_count):
    width = src_desc.shape[1]
    own_clusters = src_desc.shape[0] // CLUSTER
    key_size = lax.axis_size("key")
    src_clusters = own_clusters * key_size
    tgt_clusters = tgt_desc.shape[0] // CLUSTER
    slot_total = pair_blocks.shape[3]
    ids = pair_blocks.reshape(2, slot_total)
    cnt = pair_count.reshape(1)

    group_src = lax.all_gather(src_desc, "key", axis=0, tiled=True)
    sq_src = (jnp.sum(group_src.astype(jnp.float32) ** 2, axis=1) / width).reshape(src_clusters, CLUSTER)

    sq_tgt = (jnp.sum(tgt_desc.astype(jnp.float32) ** 2, axis=1) / width).reshape(-1, 1)
    pot_col = tgt_dual.reshape(-1, 1)

    src_shape = jax.ShapeDtypeStruct((src_clusters, CLUSTER), jnp.float32)
    src_tops, src_totals = _sweep(
        _first_kernel, src_shape, ids, cnt, group_src, tgt_desc, sq_src, sq_tgt, pot_col
    )
    key_index = lax.axis_index("key")
    own_rows = lax.broadcasted_iota(jnp.int32, (src_clusters, CLUSTER), 0) // own_clusters == key_index
    own_weight = jnp.tile(src_weight.reshape(own_clusters, CLUSTER), (key_size, 1))
    weight_rows = jnp.where(own_rows, own_weight, jnp.zeros_like(own_weight))
    full_top, full_total, group_weight = butterfly(
        jnp.stack([src_tops, src_totals, weight_rows]), "key", key_size, key_index
    )
    group_lse = full_top + jnp.log(full_total)
    group_dual = ENTROPY * jnp.log(group_weight) - ENTROPY * group_lse
    share_start = key_index * own_clusters
    src_dual = lax.dynamic_slice_in_dim(group_dual, share_start, own_clusters, 0).reshape(-1)

    tgt_shape = jax.ShapeDtypeStruct((tgt_clusters * CLUSTER, 1), jnp.float32)
    tgt_tops, tgt_totals = _sweep(
        _second_kernel, tgt_shape, ids, cnt, group_src, tgt_desc, sq_src, sq_tgt, group_dual
    )
    tgt_pack = jnp.stack([tgt_tops.reshape(tgt_clusters, CLUSTER), tgt_totals.reshape(tgt_clusters, CLUSTER)])
    all_pack = lax.all_gather(tgt_pack, "group", axis=0)
    tops4 = all_pack[:, 0]
    tots4 = all_pack[:, 1]
    merged_top = jnp.max(tops4, axis=0)
    merged_total = jnp.sum(tots4 * jnp.exp(tops4 - merged_top[None]), axis=0)
    tgt_lse = (merged_top + jnp.log(merged_total)).reshape(-1)
    tgt_dual_new = ENTROPY * jnp.log(tgt_weight) - ENTROPY * tgt_lse
    return (src_dual, tgt_dual_new)


def solution(mesh):
    in_specs = (
        P(("group", "key"), None),
        P("key", None),
        P(("group", "key")),
        P("key"),
        P("key"),
        P("group", "key", None, None),
        P("group", "key"),
    )
    out_specs = (P(("group", "key")), P("key"))
    return jax.shard_map(local, mesh=mesh, in_specs=in_specs, out_specs=out_specs, check_vma=False)
```

```python
import functools

import jax
import jax.numpy as jnp
from jax import lax
from jax.experimental import pallas as pl
from jax.experimental.pallas import tpu as pltpu
from jax.sharding import PartitionSpec as P

CLUSTER = 256
UNROLL = 4

ENTROPY = 0.05
INV_ENTROPY = 20.0
NEG_FLOOR = -1e30


def _slot_ids(ids_ref, slot, src_clusters, tgt_clusters):
    src_id = jnp.minimum(jnp.maximum(ids_ref[0, slot], 0), src_clusters - 1)
    tgt_id = jnp.minimum(jnp.maximum(ids_ref[1, slot], 0), tgt_clusters - 1)
    return src_id, tgt_id


def _block_cost(src_ref, tgt_ref, sqs_ref, sqt_ref, src_id, tgt_id, width):
    src_start = pl.multiple_of(src_id * CLUSTER, CLUSTER)
    tgt_start = pl.multiple_of(tgt_id * CLUSTER, CLUSTER)
    src_rows = src_ref[pl.ds(src_start, CLUSTER), :]
    tgt_rows = tgt_ref[pl.ds(tgt_start, CLUSTER), :]
    inner = lax.dot_general(
        tgt_rows, src_rows, (((1,), (1,)), ((), ())), preferred_element_type=jnp.float32
    )
    sq_s = sqs_ref[pl.ds(src_id, 1), :]
    sq_t = sqt_ref[pl.ds(tgt_start, CLUSTER), :]
    return (sq_s + sq_t) - (2.0 / width) * inner


def _first_kernel(ids_ref, cnt_ref, src_ref, tgt_ref, sqs_ref, sqt_ref, pot_ref, top_ref, tot_ref):
    src_clusters = sqs_ref.shape[0]
    tgt_clusters = tgt_ref.shape[0] // CLUSTER
    width = src_ref.shape[1]
    top_ref[...] = jnp.full(top_ref.shape, NEG_FLOOR, jnp.float32)
    tot_ref[...] = jnp.zeros(tot_ref.shape, jnp.float32)
    count = jnp.minimum(jnp.maximum(cnt_ref[0], 0), ids_ref.shape[1])

    def scores_of(slot):
        src_id, tgt_id = _slot_ids(ids_ref, slot, src_clusters, tgt_clusters)
        cost = _block_cost(src_ref, tgt_ref, sqs_ref, sqt_ref, src_id, tgt_id, width)
        pot = pot_ref[pl.ds(pl.multiple_of(tgt_id * CLUSTER, CLUSTER), CLUSTER), :]
        return src_id, (pot - cost) * INV_ENTROPY

    def update(src_id, scores):
        peak = jnp.max(scores, axis=0, keepdims=True)
        old_top = top_ref[pl.ds(src_id, 1), :]
        old_tot = tot_ref[pl.ds(src_id, 1), :]
        new_top = jnp.maximum(old_top, peak)
        new_tot = old_tot * jnp.exp(old_top - new_top) + jnp.sum(
            jnp.exp(scores - new_top), axis=0, keepdims=True
        )
        top_ref[pl.ds(src_id, 1), :] = new_top
        tot_ref[pl.ds(src_id, 1), :] = new_tot

    def body(trip, carry):
        blocks = [scores_of(UNROLL * trip + lane) for lane in range(UNROLL)]
        for block in blocks:
            update(*block)
        return carry

    def tail(slot, carry):
        update(*scores_of(slot))
        return carry

    lax.fori_loop(0, count // UNROLL, body, 0)
    lax.fori_loop(count // UNROLL * UNROLL, count, tail, 0)


def _second_kernel(ids_ref, cnt_ref, src_ref, tgt_ref, sqs_ref, sqt_ref, dual_ref, top_ref, tot_ref):
    src_clusters = sqs_ref.shape[0]
    tgt_clusters = tgt_ref.shape[0] // CLUSTER
    width = src_ref.shape[1]
    top_ref[...] = jnp.full(top_ref.shape, NEG_FLOOR, jnp.float32)
    tot_ref[...] = jnp.zeros(tot_ref.shape, jnp.float32)
    count = jnp.minimum(jnp.maximum(cnt_ref[0], 0), ids_ref.shape[1])

    def scores_of(slot):
        src_id, tgt_id = _slot_ids(ids_ref, slot, src_clusters, tgt_clusters)
        cost = _block_cost(src_ref, tgt_ref, sqs_ref, sqt_ref, src_id, tgt_id, width)
        pot = dual_ref[pl.ds(src_id, 1), :]
        return tgt_id, (pot - cost) * INV_ENTROPY

    def update(tgt_id, scores):
        peak = jnp.max(scores, axis=1, keepdims=True)
        tgt_rows = pl.ds(pl.multiple_of(tgt_id * CLUSTER, CLUSTER), CLUSTER)
        old_top = top_ref[tgt_rows, :]
        old_tot = tot_ref[tgt_rows, :]
        new_top = jnp.maximum(old_top, peak)
        new_tot = old_tot * jnp.exp(old_top - new_top) + jnp.sum(
            jnp.exp(scores - new_top), axis=1, keepdims=True
        )
        top_ref[tgt_rows, :] = new_top
        tot_ref[tgt_rows, :] = new_tot

    def body(trip, carry):
        blocks = [scores_of(UNROLL * trip + lane) for lane in range(UNROLL)]
        for block in blocks:
            update(*block)
        return carry

    def tail(slot, carry):
        update(*scores_of(slot))
        return carry

    lax.fori_loop(0, count // UNROLL, body, 0)
    lax.fori_loop(count // UNROLL * UNROLL, count, tail, 0)


def _sweep(kernel, out_shape, ids, cnt, group_src, tgt_desc, sq_src, sq_tgt, pot):
    vmem = pl.BlockSpec(memory_space=pltpu.VMEM)
    smem = pl.BlockSpec(memory_space=pltpu.SMEM)
    slots = ids.shape[1]
    flops = 2 * slots * CLUSTER * CLUSTER * group_src.shape[1]
    return pl.pallas_call(
        kernel,
        out_shape=(out_shape, out_shape),
        in_specs=[smem, smem, vmem, vmem, vmem, vmem, vmem],
        out_specs=(vmem, vmem),
        compiler_params=pltpu.CompilerParams(vmem_limit_bytes=48 * 1024 * 1024),
        cost_estimate=pl.CostEstimate(
            flops=flops,
            transcendentals=slots * CLUSTER * CLUSTER,
            bytes_accessed=group_src.size * 2 + tgt_desc.size * 2,
        ),
    )(ids, cnt, group_src, tgt_desc, sq_src, sq_tgt, pot)


def merge_lse(first, second):
    top = jnp.maximum(first, second)
    return top + jnp.log1p(jnp.exp(jnp.minimum(first, second) - top))


def butterfly(lse, weight, axis, size, index):
    bit = 1
    rows = lse.shape[0]
    while bit < size:
        perm = [(i, i ^ bit) for i in range(size)]
        other = lax.ppermute(jnp.concatenate([lse, weight], axis=0), axis, perm)
        lse = merge_lse(lse, other[:rows])
        is_low = (index & bit) == 0
        low = jnp.where(is_low, weight, other[rows:])
        high = jnp.where(is_low, other[rows:], weight)
        weight = jnp.concatenate([low, high], axis=0)
        bit *= 2
    return lse, weight


def local(src_desc, tgt_desc, src_weight, tgt_weight, tgt_dual, pair_blocks, pair_count):
    width = src_desc.shape[1]
    own_clusters = src_desc.shape[0] // CLUSTER
    key_size = lax.axis_size("key")
    src_clusters = own_clusters * key_size
    tgt_clusters = tgt_desc.shape[0] // CLUSTER
    slot_total = pair_blocks.shape[3]
    ids = pair_blocks.reshape(2, slot_total)
    cnt = pair_count.reshape(1)

    group_src = lax.all_gather(src_desc, "key", axis=0, tiled=True)
    sq_src = (jnp.sum(group_src.astype(jnp.float32) ** 2, axis=1) / width).reshape(src_clusters, CLUSTER)

    sq_tgt = (jnp.sum(tgt_desc.astype(jnp.float32) ** 2, axis=1) / width).reshape(-1, 1)
    pot_col = tgt_dual.reshape(-1, 1)

    src_shape = jax.ShapeDtypeStruct((src_clusters, CLUSTER), jnp.float32)
    src_tops, src_totals = _sweep(
        _first_kernel, src_shape, ids, cnt, group_src, tgt_desc, sq_src, sq_tgt, pot_col
    )
    key_index = lax.axis_index("key")
    local_lse = jnp.maximum(src_tops + jnp.log(src_totals), NEG_FLOOR)
    group_lse, group_weight = butterfly(
        local_lse, src_weight.reshape(own_clusters, CLUSTER), "key", key_size, key_index
    )
    group_dual = ENTROPY * jnp.log(group_weight) - ENTROPY * group_lse
    share_start = key_index * own_clusters
    src_dual = lax.dynamic_slice_in_dim(group_dual, share_start, own_clusters, 0).reshape(-1)

    tgt_shape = jax.ShapeDtypeStruct((tgt_clusters * CLUSTER, 1), jnp.float32)
    tgt_tops, tgt_totals = _sweep(
        _second_kernel, tgt_shape, ids, cnt, group_src, tgt_desc, sq_src, sq_tgt, group_dual
    )
    tgt_pack = jnp.stack([tgt_tops.reshape(tgt_clusters, CLUSTER), tgt_totals.reshape(tgt_clusters, CLUSTER)])
    all_pack = lax.all_gather(tgt_pack, "group", axis=0)
    tops4 = all_pack[:, 0]
    tots4 = all_pack[:, 1]
    merged_top = jnp.max(tops4, axis=0)
    merged_total = jnp.sum(tots4 * jnp.exp(tops4 - merged_top[None]), axis=0)
    tgt_lse = (merged_top + jnp.log(merged_total)).reshape(-1)
    tgt_dual_new = ENTROPY * jnp.log(tgt_weight) - ENTROPY * tgt_lse
    return (src_dual, tgt_dual_new)


def solution(mesh):
    in_specs = (
        P(("group", "key"), None),
        P("key", None),
        P(("group", "key")),
        P("key"),
        P("key"),
        P("group", "key", None, None),
        P("group", "key"),
    )
    out_specs = (P(("group", "key")), P("key"))
    return jax.shard_map(local, mesh=mesh, in_specs=in_specs, out_specs=out_specs, check_vma=False)
```

```python
import functools

import jax
import jax.numpy as jnp
from jax import lax
from jax.experimental import pallas as pl
from jax.experimental.pallas import tpu as pltpu
from jax.sharding import PartitionSpec as P

CLUSTER = 256
UNROLL = 4

ENTROPY = 0.05
INV_ENTROPY = 20.0
NEG_FLOOR = -1e30


def _slot_ids(ids_ref, slot, src_clusters, tgt_clusters):
    src_id = jnp.minimum(jnp.maximum(ids_ref[0, slot], 0), src_clusters - 1)
    tgt_id = jnp.minimum(jnp.maximum(ids_ref[1, slot], 0), tgt_clusters - 1)
    return src_id, tgt_id


def _block_cost(src_rows, tgt_ref, sqs_ref, sqt_ref, src_id, tgt_id, width):
    tgt_start = pl.multiple_of(tgt_id * CLUSTER, CLUSTER)
    tgt_rows = tgt_ref[pl.ds(tgt_start, CLUSTER), :]
    inner = lax.dot_general(
        tgt_rows, src_rows, (((1,), (1,)), ((), ())), preferred_element_type=jnp.float32
    )
    sq_s = sqs_ref[pl.ds(src_id, 1), :]
    sq_t = sqt_ref[pl.ds(tgt_start, CLUSTER), :]
    return (sq_s + sq_t) - (2.0 / width) * inner


def _drive(ids_ref, cnt_ref, src_hbm, src_buf, sems, src_clusters, scores_of, update):
    count = jnp.minimum(jnp.maximum(cnt_ref[0], 0), ids_ref.shape[1])
    trips = count // UNROLL

    def copy(slot, buf):
        src_id = jnp.minimum(jnp.maximum(ids_ref[0, slot], 0), src_clusters - 1)
        start = pl.multiple_of(src_id * CLUSTER, CLUSTER)
        return pltpu.make_async_copy(src_hbm.at[pl.ds(start, CLUSTER)], src_buf.at[buf], sems.at[buf])

    @pl.when(trips > 0)
    def _():
        for lane in range(UNROLL):
            copy(lane, lane).start()

    def body(trip, carry):
        base = (trip % 2) * UNROLL
        for lane in range(UNROLL):
            copy(UNROLL * trip + lane, base + lane).wait()

        @pl.when(trip + 1 < trips)
        def _():
            ahead = UNROLL - base
            for lane in range(UNROLL):
                copy(UNROLL * (trip + 1) + lane, ahead + lane).start()

        blocks = [scores_of(UNROLL * trip + lane, base + lane) for lane in range(UNROLL)]
        for block in blocks:
            update(*block)
        return carry

    def tail(slot, carry):
        single = copy(slot, 0)
        single.start()
        single.wait()
        update(*scores_of(slot, 0))
        return carry

    lax.fori_loop(0, trips, body, 0)
    lax.fori_loop(trips * UNROLL, count, tail, 0)


def _first_kernel(ids_ref, cnt_ref, src_hbm, tgt_ref, sqs_ref, sqt_ref, pot_ref, top_ref, tot_ref, src_buf, sems):
    src_clusters = sqs_ref.shape[0]
    tgt_clusters = tgt_ref.shape[0] // CLUSTER
    width = src_hbm.shape[1]
    top_ref[...] = jnp.full(top_ref.shape, NEG_FLOOR, jnp.float32)
    tot_ref[...] = jnp.zeros(tot_ref.shape, jnp.float32)

    def scores_of(slot, buf):
        src_id, tgt_id = _slot_ids(ids_ref, slot, src_clusters, tgt_clusters)
        cost = _block_cost(src_buf[buf], tgt_ref, sqs_ref, sqt_ref, src_id, tgt_id, width)
        pot = pot_ref[pl.ds(pl.multiple_of(tgt_id * CLUSTER, CLUSTER), CLUSTER), :]
        return src_id, (pot - cost) * INV_ENTROPY

    def update(src_id, scores):
        peak = jnp.max(scores, axis=0, keepdims=True)
        old_top = top_ref[pl.ds(src_id, 1), :]
        old_tot = tot_ref[pl.ds(src_id, 1), :]
        new_top = jnp.maximum(old_top, peak)
        new_tot = old_tot * jnp.exp(old_top - new_top) + jnp.sum(
            jnp.exp(scores - new_top), axis=0, keepdims=True
        )
        top_ref[pl.ds(src_id, 1), :] = new_top
        tot_ref[pl.ds(src_id, 1), :] = new_tot

    _drive(ids_ref, cnt_ref, src_hbm, src_buf, sems, src_clusters, scores_of, update)


def _second_kernel(ids_ref, cnt_ref, src_hbm, tgt_ref, sqs_ref, sqt_ref, dual_ref, top_ref, tot_ref, src_buf, sems):
    src_clusters = sqs_ref.shape[0]
    tgt_clusters = tgt_ref.shape[0] // CLUSTER
    width = src_hbm.shape[1]
    top_ref[...] = jnp.full(top_ref.shape, NEG_FLOOR, jnp.float32)
    tot_ref[...] = jnp.zeros(tot_ref.shape, jnp.float32)

    def scores_of(slot, buf):
        src_id, tgt_id = _slot_ids(ids_ref, slot, src_clusters, tgt_clusters)
        cost = _block_cost(src_buf[buf], tgt_ref, sqs_ref, sqt_ref, src_id, tgt_id, width)
        pot = dual_ref[pl.ds(src_id, 1), :]
        return tgt_id, (pot - cost) * INV_ENTROPY

    def update(tgt_id, scores):
        peak = jnp.max(scores, axis=1, keepdims=True)
        tgt_rows = pl.ds(pl.multiple_of(tgt_id * CLUSTER, CLUSTER), CLUSTER)
        old_top = top_ref[tgt_rows, :]
        old_tot = tot_ref[tgt_rows, :]
        new_top = jnp.maximum(old_top, peak)
        new_tot = old_tot * jnp.exp(old_top - new_top) + jnp.sum(
            jnp.exp(scores - new_top), axis=1, keepdims=True
        )
        top_ref[tgt_rows, :] = new_top
        tot_ref[tgt_rows, :] = new_tot

    _drive(ids_ref, cnt_ref, src_hbm, src_buf, sems, src_clusters, scores_of, update)


def _sweep(kernel, out_shape, ids, cnt, group_src, tgt_desc, sq_src, sq_tgt, pot):
    vmem = pl.BlockSpec(memory_space=pltpu.VMEM)
    smem = pl.BlockSpec(memory_space=pltpu.SMEM)
    hbm = pl.BlockSpec(memory_space=pl.ANY)
    slots = ids.shape[1]
    width = group_src.shape[1]
    flops = 2 * slots * CLUSTER * CLUSTER * width
    return pl.pallas_call(
        kernel,
        out_shape=(out_shape, out_shape),
        in_specs=[smem, smem, hbm, vmem, vmem, vmem, vmem],
        out_specs=(vmem, vmem),
        scratch_shapes=[
            pltpu.VMEM((2 * UNROLL, CLUSTER, width), group_src.dtype),
            pltpu.SemaphoreType.DMA((2 * UNROLL,)),
        ],
        compiler_params=pltpu.CompilerParams(vmem_limit_bytes=32 * 1024 * 1024),
        cost_estimate=pl.CostEstimate(
            flops=flops,
            transcendentals=slots * CLUSTER * CLUSTER,
            bytes_accessed=slots * CLUSTER * width * 2 + tgt_desc.size * 2,
        ),
    )(ids, cnt, group_src, tgt_desc, sq_src, sq_tgt, pot)


def merge_lse(first, second):
    top = jnp.maximum(first, second)
    return top + jnp.log1p(jnp.exp(jnp.minimum(first, second) - top))


def butterfly(lse, weight, axis, size, index):
    bit = 1
    rows = lse.shape[0]
    while bit < size:
        perm = [(i, i ^ bit) for i in range(size)]
        other = lax.ppermute(jnp.concatenate([lse, weight], axis=0), axis, perm)
        lse = merge_lse(lse, other[:rows])
        is_low = (index & bit) == 0
        low = jnp.where(is_low, weight, other[rows:])
        high = jnp.where(is_low, other[rows:], weight)
        weight = jnp.concatenate([low, high], axis=0)
        bit *= 2
    return lse, weight


def local(src_desc, tgt_desc, src_weight, tgt_weight, tgt_dual, pair_blocks, pair_count):
    width = src_desc.shape[1]
    own_clusters = src_desc.shape[0] // CLUSTER
    key_size = lax.axis_size("key")
    src_clusters = own_clusters * key_size
    tgt_clusters = tgt_desc.shape[0] // CLUSTER
    slot_total = pair_blocks.shape[3]
    ids = pair_blocks.reshape(2, slot_total)
    cnt = pair_count.reshape(1)

    group_src = lax.all_gather(src_desc, "key", axis=0, tiled=True)
    sq_src = (jnp.sum(group_src.astype(jnp.float32) ** 2, axis=1) / width).reshape(src_clusters, CLUSTER)

    sq_tgt = (jnp.sum(tgt_desc.astype(jnp.float32) ** 2, axis=1) / width).reshape(-1, 1)
    pot_col = tgt_dual.reshape(-1, 1)

    src_shape = jax.ShapeDtypeStruct((src_clusters, CLUSTER), jnp.float32)
    src_tops, src_totals = _sweep(
        _first_kernel, src_shape, ids, cnt, group_src, tgt_desc, sq_src, sq_tgt, pot_col
    )
    key_index = lax.axis_index("key")
    local_lse = jnp.maximum(src_tops + jnp.log(src_totals), NEG_FLOOR)
    group_lse, group_weight = butterfly(
        local_lse, src_weight.reshape(own_clusters, CLUSTER), "key", key_size, key_index
    )
    group_dual = ENTROPY * jnp.log(group_weight) - ENTROPY * group_lse
    share_start = key_index * own_clusters
    src_dual = lax.dynamic_slice_in_dim(group_dual, share_start, own_clusters, 0).reshape(-1)

    tgt_shape = jax.ShapeDtypeStruct((tgt_clusters * CLUSTER, 1), jnp.float32)
    tgt_tops, tgt_totals = _sweep(
        _second_kernel, tgt_shape, ids, cnt, group_src, tgt_desc, sq_src, sq_tgt, group_dual
    )
    tgt_pack = jnp.stack([tgt_tops.reshape(tgt_clusters, CLUSTER), tgt_totals.reshape(tgt_clusters, CLUSTER)])
    all_pack = lax.all_gather(tgt_pack, "group", axis=0)
    tops4 = all_pack[:, 0]
    tots4 = all_pack[:, 1]
    merged_top = jnp.max(tops4, axis=0)
    merged_total = jnp.sum(tots4 * jnp.exp(tops4 - merged_top[None]), axis=0)
    tgt_lse = (merged_top + jnp.log(merged_total)).reshape(-1)
    tgt_dual_new = ENTROPY * jnp.log(tgt_weight) - ENTROPY * tgt_lse
    return (src_dual, tgt_dual_new)


def solution(mesh):
    in_specs = (
        P(("group", "key"), None),
        P("key", None),
        P(("group", "key")),
        P("key"),
        P("key"),
        P("group", "key", None, None),
        P("group", "key"),
    )
    out_specs = (P(("group", "key")), P("key"))
    return jax.shard_map(local, mesh=mesh, in_specs=in_specs, out_specs=out_specs, check_vma=False)
```

```python
import functools

import jax
import jax.numpy as jnp
from jax import lax
from jax.experimental import pallas as pl
from jax.experimental.pallas import tpu as pltpu
from jax.sharding import PartitionSpec as P

CLUSTER = 256
UNROLL = 4

ENTROPY = 0.05
INV_ENTROPY = 20.0
NEG_FLOOR = -1e30


def _slot_ids(ids_ref, slot, src_clusters, tgt_clusters):
    src_id = jnp.minimum(jnp.maximum(ids_ref[0, slot], 0), src_clusters - 1)
    tgt_id = jnp.minimum(jnp.maximum(ids_ref[1, slot], 0), tgt_clusters - 1)
    return src_id, tgt_id


def _block_cost(src_ref, tgt_ref, sqs_ref, sqt_ref, src_id, tgt_id, width):
    src_start = pl.multiple_of(src_id * CLUSTER, CLUSTER)
    tgt_start = pl.multiple_of(tgt_id * CLUSTER, CLUSTER)
    src_rows = src_ref[pl.ds(src_start, CLUSTER), :]
    tgt_rows = tgt_ref[pl.ds(tgt_start, CLUSTER), :]
    inner = lax.dot_general(
        tgt_rows, src_rows, (((1,), (1,)), ((), ())), preferred_element_type=jnp.float32
    )
    sq_s = sqs_ref[pl.ds(src_id, 1), :]
    sq_t = sqt_ref[pl.ds(tgt_start, CLUSTER), :]
    return (sq_s + sq_t) - (2.0 / width) * inner


def _first_kernel(ids_ref, cnt_ref, src_ref, tgt_ref, sqs_ref, sqt_ref, pot_ref, top_ref, tot_ref):
    src_clusters = sqs_ref.shape[0]
    tgt_clusters = tgt_ref.shape[0] // CLUSTER
    width = src_ref.shape[1]
    top_ref[...] = jnp.full(top_ref.shape, NEG_FLOOR, jnp.float32)
    tot_ref[...] = jnp.zeros(tot_ref.shape, jnp.float32)
    count = jnp.minimum(jnp.maximum(cnt_ref[0], 0), ids_ref.shape[1])

    def scores_of(slot):
        src_id, tgt_id = _slot_ids(ids_ref, slot, src_clusters, tgt_clusters)
        cost = _block_cost(src_ref, tgt_ref, sqs_ref, sqt_ref, src_id, tgt_id, width)
        pot = pot_ref[pl.ds(pl.multiple_of(tgt_id * CLUSTER, CLUSTER), CLUSTER), :]
        return src_id, (pot - cost) * INV_ENTROPY

    def update(src_id, scores):
        peak = jnp.max(scores, axis=0, keepdims=True)
        old_top = top_ref[pl.ds(src_id, 1), :]
        old_tot = tot_ref[pl.ds(src_id, 1), :]
        new_top = jnp.maximum(old_top, peak)
        new_tot = old_tot * jnp.exp(old_top - new_top) + jnp.sum(
            jnp.exp(scores - new_top), axis=0, keepdims=True
        )
        top_ref[pl.ds(src_id, 1), :] = new_top
        tot_ref[pl.ds(src_id, 1), :] = new_tot

    def body(trip, carry):
        blocks = [scores_of(UNROLL * trip + lane) for lane in range(UNROLL)]
        for block in blocks:
            update(*block)
        return carry

    def tail(slot, carry):
        update(*scores_of(slot))
        return carry

    lax.fori_loop(0, count // UNROLL, body, 0)
    lax.fori_loop(count // UNROLL * UNROLL, count, tail, 0)
    top_ref[...] = jnp.maximum(top_ref[...] + jnp.log(tot_ref[...]), NEG_FLOOR)


def _second_kernel(ids_ref, cnt_ref, src_ref, tgt_ref, sqs_ref, sqt_ref, dual_ref, lse_ref, top_ref, tot_ref):
    src_clusters = sqs_ref.shape[0]
    tgt_clusters = tgt_ref.shape[0] // CLUSTER
    width = src_ref.shape[1]
    top_ref[...] = jnp.full(top_ref.shape, NEG_FLOOR, jnp.float32)
    tot_ref[...] = jnp.zeros(tot_ref.shape, jnp.float32)
    count = jnp.minimum(jnp.maximum(cnt_ref[0], 0), ids_ref.shape[1])

    def scores_of(slot):
        src_id, tgt_id = _slot_ids(ids_ref, slot, src_clusters, tgt_clusters)
        cost = _block_cost(src_ref, tgt_ref, sqs_ref, sqt_ref, src_id, tgt_id, width)
        pot = dual_ref[pl.ds(src_id, 1), :]
        return tgt_id, (pot - cost) * INV_ENTROPY

    def update(tgt_id, scores):
        peak = jnp.max(scores, axis=1, keepdims=True)
        tgt_rows = pl.ds(pl.multiple_of(tgt_id * CLUSTER, CLUSTER), CLUSTER)
        old_top = top_ref[tgt_rows, :]
        old_tot = tot_ref[tgt_rows, :]
        new_top = jnp.maximum(old_top, peak)
        new_tot = old_tot * jnp.exp(old_top - new_top) + jnp.sum(
            jnp.exp(scores - new_top), axis=1, keepdims=True
        )
        top_ref[tgt_rows, :] = new_top
        tot_ref[tgt_rows, :] = new_tot

    def body(trip, carry):
        blocks = [scores_of(UNROLL * trip + lane) for lane in range(UNROLL)]
        for block in blocks:
            update(*block)
        return carry

    def tail(slot, carry):
        update(*scores_of(slot))
        return carry

    lax.fori_loop(0, count // UNROLL, body, 0)
    lax.fori_loop(count // UNROLL * UNROLL, count, tail, 0)
    for cluster in range(tgt_clusters):
        rows = pl.ds(cluster * CLUSTER, CLUSTER)
        column = jnp.maximum(top_ref[rows, :] + jnp.log(tot_ref[rows, :]), NEG_FLOOR)
        wide = jnp.broadcast_to(column, (CLUSTER, 128))
        lse_ref[pl.ds(cluster, 1), :] = jnp.transpose(wide)[0:1, :]


def _sweep(kernel, out_shapes, scratch, ids, cnt, group_src, tgt_desc, sq_src, sq_tgt, pot):
    vmem = pl.BlockSpec(memory_space=pltpu.VMEM)
    smem = pl.BlockSpec(memory_space=pltpu.SMEM)
    slots = ids.shape[1]
    flops = 2 * slots * CLUSTER * CLUSTER * group_src.shape[1]
    return pl.pallas_call(
        kernel,
        out_shape=out_shapes,
        in_specs=[smem, smem, vmem, vmem, vmem, vmem, vmem],
        out_specs=tuple(vmem for _ in out_shapes),
        scratch_shapes=scratch,
        compiler_params=pltpu.CompilerParams(vmem_limit_bytes=48 * 1024 * 1024),
        cost_estimate=pl.CostEstimate(
            flops=flops,
            transcendentals=slots * CLUSTER * CLUSTER,
            bytes_accessed=group_src.size * 2 + tgt_desc.size * 2,
        ),
    )(ids, cnt, group_src, tgt_desc, sq_src, sq_tgt, pot)


def merge_lse(first, second):
    top = jnp.maximum(first, second)
    return top + jnp.log1p(jnp.exp(jnp.minimum(first, second) - top))


def butterfly(lse, weight, axis, size, index):
    bit = 1
    rows = lse.shape[0]
    while bit < size:
        perm = [(i, i ^ bit) for i in range(size)]
        other = lax.ppermute(jnp.concatenate([lse, weight], axis=0), axis, perm)
        lse = merge_lse(lse, other[:rows])
        is_low = (index & bit) == 0
        low = jnp.where(is_low, weight, other[rows:])
        high = jnp.where(is_low, other[rows:], weight)
        weight = jnp.concatenate([low, high], axis=0)
        bit *= 2
    return lse, weight


def local(src_desc, tgt_desc, src_weight, tgt_weight, tgt_dual, pair_blocks, pair_count):
    width = src_desc.shape[1]
    own_clusters = src_desc.shape[0] // CLUSTER
    key_size = lax.axis_size("key")
    src_clusters = own_clusters * key_size
    tgt_clusters = tgt_desc.shape[0] // CLUSTER
    slot_total = pair_blocks.shape[3]
    ids = pair_blocks.reshape(2, slot_total)
    cnt = pair_count.reshape(1)

    group_src = lax.all_gather(src_desc, "key", axis=0, tiled=True)
    sq_src = (jnp.sum(group_src.astype(jnp.float32) ** 2, axis=1) / width).reshape(src_clusters, CLUSTER)

    sq_tgt = (jnp.sum(tgt_desc.astype(jnp.float32) ** 2, axis=1) / width).reshape(-1, 1)
    pot_col = tgt_dual.reshape(-1, 1)

    src_shape = jax.ShapeDtypeStruct((src_clusters, CLUSTER), jnp.float32)
    local_lse, _ = _sweep(
        _first_kernel, (src_shape, src_shape), [], ids, cnt, group_src, tgt_desc, sq_src, sq_tgt, pot_col
    )
    key_index = lax.axis_index("key")
    group_lse, group_weight = butterfly(
        local_lse, src_weight.reshape(own_clusters, CLUSTER), "key", key_size, key_index
    )
    group_dual = ENTROPY * jnp.log(group_weight) - ENTROPY * group_lse
    share_start = key_index * own_clusters
    src_dual = lax.dynamic_slice_in_dim(group_dual, share_start, own_clusters, 0).reshape(-1)

    tgt_shape = jax.ShapeDtypeStruct((tgt_clusters, CLUSTER), jnp.float32)
    column = pltpu.VMEM((tgt_clusters * CLUSTER, 1), jnp.float32)
    (tgt_part,) = _sweep(
        _second_kernel, (tgt_shape,), [column, column], ids, cnt, group_src, tgt_desc, sq_src, sq_tgt, group_dual
    )
    parts = lax.all_gather(tgt_part, "group", axis=0)
    merged = parts[0]
    for index in range(1, parts.shape[0]):
        merged = merge_lse(merged, parts[index])
    tgt_lse = merged.reshape(-1)
    tgt_dual_new = ENTROPY * jnp.log(tgt_weight) - ENTROPY * tgt_lse
    return (src_dual, tgt_dual_new)


def solution(mesh):
    in_specs = (
        P(("group", "key"), None),
        P("key", None),
        P(("group", "key")),
        P("key"),
        P("key"),
        P("group", "key", None, None),
        P("group", "key"),
    )
    out_specs = (P(("group", "key")), P("key"))
    return jax.shard_map(local, mesh=mesh, in_specs=in_specs, out_specs=out_specs, check_vma=False)
```

```python
import functools

import jax
import jax.numpy as jnp
from jax import lax
from jax.experimental import pallas as pl
from jax.experimental.pallas import tpu as pltpu
from jax.sharding import PartitionSpec as P

CLUSTER = 256
UNROLL = 4

ENTROPY = 0.05
INV_ENTROPY = 20.0
NEG_FLOOR = -1e30


def _slot_ids(ids_ref, slot, src_clusters, tgt_clusters):
    src_id = jnp.minimum(jnp.maximum(ids_ref[0, slot], 0), src_clusters - 1)
    tgt_id = jnp.minimum(jnp.maximum(ids_ref[1, slot], 0), tgt_clusters - 1)
    return src_id, tgt_id


def _block_cost(src_ref, tgt_ref, sqs_ref, sqt_ref, src_id, tgt_id, width):
    src_start = pl.multiple_of(src_id * CLUSTER, CLUSTER)
    tgt_start = pl.multiple_of(tgt_id * CLUSTER, CLUSTER)
    src_rows = src_ref[pl.ds(src_start, CLUSTER), :]
    tgt_rows = tgt_ref[pl.ds(tgt_start, CLUSTER), :]
    inner = lax.dot_general(
        tgt_rows, src_rows, (((1,), (1,)), ((), ())), preferred_element_type=jnp.float32
    )
    sq_s = sqs_ref[pl.ds(src_id, 1), :]
    sq_t = sqt_ref[pl.ds(tgt_start, CLUSTER), :]
    return (sq_s + sq_t) - (2.0 / width) * inner


def _first_kernel(ids_ref, cnt_ref, src_ref, tgt_ref, sqs_ref, sqt_ref, pot_ref, top_ref, tot_ref):
    src_clusters = sqs_ref.shape[0]
    tgt_clusters = tgt_ref.shape[0] // CLUSTER
    width = src_ref.shape[1]
    top_ref[...] = jnp.full(top_ref.shape, NEG_FLOOR, jnp.float32)
    tot_ref[...] = jnp.zeros(tot_ref.shape, jnp.float32)
    count = jnp.minimum(jnp.maximum(cnt_ref[0], 0), ids_ref.shape[1])

    def scores_of(slot):
        src_id, tgt_id = _slot_ids(ids_ref, slot, src_clusters, tgt_clusters)
        cost = _block_cost(src_ref, tgt_ref, sqs_ref, sqt_ref, src_id, tgt_id, width)
        pot = pot_ref[pl.ds(pl.multiple_of(tgt_id * CLUSTER, CLUSTER), CLUSTER), :]
        return src_id, (pot - cost) * INV_ENTROPY

    def update(src_id, scores):
        peak = jnp.max(scores, axis=0, keepdims=True)
        old_top = top_ref[pl.ds(src_id, 1), :]
        old_tot = tot_ref[pl.ds(src_id, 1), :]
        new_top = jnp.maximum(old_top, peak)
        new_tot = old_tot * jnp.exp(old_top - new_top) + jnp.sum(
            jnp.exp(scores - new_top), axis=0, keepdims=True
        )
        top_ref[pl.ds(src_id, 1), :] = new_top
        tot_ref[pl.ds(src_id, 1), :] = new_tot

    def body(trip, carry):
        blocks = [scores_of(UNROLL * trip + lane) for lane in range(UNROLL)]
        for block in blocks:
            update(*block)
        return carry

    def tail(slot, carry):
        update(*scores_of(slot))
        return carry

    lax.fori_loop(0, count // UNROLL, body, 0)
    lax.fori_loop(count // UNROLL * UNROLL, count, tail, 0)
    top_ref[...] = jnp.maximum(top_ref[...] + jnp.log(tot_ref[...]), NEG_FLOOR)


def _second_kernel(ids_ref, cnt_ref, src_ref, tgt_ref, sqs_ref, sqt_ref, dual_ref, lse_ref, top_ref, tot_ref):
    src_clusters = sqs_ref.shape[0]
    tgt_clusters = tgt_ref.shape[0] // CLUSTER
    width = src_ref.shape[1]
    lanes = top_ref.shape[1]
    top_ref[...] = jnp.full(top_ref.shape, NEG_FLOOR, jnp.float32)
    tot_ref[...] = jnp.zeros(tot_ref.shape, jnp.float32)
    count = jnp.minimum(jnp.maximum(cnt_ref[0], 0), ids_ref.shape[1])

    def scores_of(slot):
        src_id, tgt_id = _slot_ids(ids_ref, slot, src_clusters, tgt_clusters)
        cost = _block_cost(src_ref, tgt_ref, sqs_ref, sqt_ref, src_id, tgt_id, width)
        pot = dual_ref[pl.ds(src_id, 1), :]
        return tgt_id, (pot - cost) * INV_ENTROPY

    def update(tgt_id, scores):
        halves = [scores[:, part * lanes:(part + 1) * lanes] for part in range(CLUSTER // lanes)]
        tgt_rows = pl.ds(pl.multiple_of(tgt_id * CLUSTER, CLUSTER), CLUSTER)
        old_top = top_ref[tgt_rows, :]
        old_tot = tot_ref[tgt_rows, :]
        new_top = old_top
        for half in halves:
            new_top = jnp.maximum(new_top, half)
        new_tot = old_tot * jnp.exp(old_top - new_top)
        for half in halves:
            new_tot = new_tot + jnp.exp(half - new_top)
        top_ref[tgt_rows, :] = new_top
        tot_ref[tgt_rows, :] = new_tot

    def body(trip, carry):
        blocks = [scores_of(UNROLL * trip + lane) for lane in range(UNROLL)]
        for block in blocks:
            update(*block)
        return carry

    def tail(slot, carry):
        update(*scores_of(slot))
        return carry

    lax.fori_loop(0, count // UNROLL, body, 0)
    lax.fori_loop(count // UNROLL * UNROLL, count, tail, 0)
    for cluster in range(tgt_clusters):
        rows = pl.ds(cluster * CLUSTER, CLUSTER)
        lane_top = top_ref[rows, :]
        peak = jnp.max(lane_top, axis=1, keepdims=True)
        total = jnp.sum(tot_ref[rows, :] * jnp.exp(lane_top - peak), axis=1, keepdims=True)
        column = jnp.maximum(peak + jnp.log(total), NEG_FLOOR)
        wide = jnp.broadcast_to(column, (CLUSTER, 128))
        lse_ref[pl.ds(cluster, 1), :] = jnp.transpose(wide)[0:1, :]


def _sweep(kernel, out_shapes, scratch, ids, cnt, group_src, tgt_desc, sq_src, sq_tgt, pot):
    vmem = pl.BlockSpec(memory_space=pltpu.VMEM)
    smem = pl.BlockSpec(memory_space=pltpu.SMEM)
    slots = ids.shape[1]
    flops = 2 * slots * CLUSTER * CLUSTER * group_src.shape[1]
    return pl.pallas_call(
        kernel,
        out_shape=out_shapes,
        in_specs=[smem, smem, vmem, vmem, vmem, vmem, vmem],
        out_specs=tuple(vmem for _ in out_shapes),
        scratch_shapes=scratch,
        compiler_params=pltpu.CompilerParams(vmem_limit_bytes=48 * 1024 * 1024),
        cost_estimate=pl.CostEstimate(
            flops=flops,
            transcendentals=slots * CLUSTER * CLUSTER,
            bytes_accessed=group_src.size * 2 + tgt_desc.size * 2,
        ),
    )(ids, cnt, group_src, tgt_desc, sq_src, sq_tgt, pot)


def merge_lse(first, second):
    top = jnp.maximum(first, second)
    return top + jnp.log1p(jnp.exp(jnp.minimum(first, second) - top))


def butterfly(lse, weight, axis, size, index):
    bit = 1
    rows = lse.shape[0]
    while bit < size:
        perm = [(i, i ^ bit) for i in range(size)]
        other = lax.ppermute(jnp.concatenate([lse, weight], axis=0), axis, perm)
        lse = merge_lse(lse, other[:rows])
        is_low = (index & bit) == 0
        low = jnp.where(is_low, weight, other[rows:])
        high = jnp.where(is_low, other[rows:], weight)
        weight = jnp.concatenate([low, high], axis=0)
        bit *= 2
    return lse, weight


def local(src_desc, tgt_desc, src_weight, tgt_weight, tgt_dual, pair_blocks, pair_count):
    width = src_desc.shape[1]
    own_clusters = src_desc.shape[0] // CLUSTER
    key_size = lax.axis_size("key")
    src_clusters = own_clusters * key_size
    tgt_clusters = tgt_desc.shape[0] // CLUSTER
    slot_total = pair_blocks.shape[3]
    ids = pair_blocks.reshape(2, slot_total)
    cnt = pair_count.reshape(1)

    group_src = lax.all_gather(src_desc, "key", axis=0, tiled=True)
    sq_src = (jnp.sum(group_src.astype(jnp.float32) ** 2, axis=1) / width).reshape(src_clusters, CLUSTER)

    sq_tgt = (jnp.sum(tgt_desc.astype(jnp.float32) ** 2, axis=1) / width).reshape(-1, 1)
    pot_col = tgt_dual.reshape(-1, 1)

    src_shape = jax.ShapeDtypeStruct((src_clusters, CLUSTER), jnp.float32)
    local_lse, _ = _sweep(
        _first_kernel, (src_shape, src_shape), [], ids, cnt, group_src, tgt_desc, sq_src, sq_tgt, pot_col
    )
    key_index = lax.axis_index("key")
    group_lse, group_weight = butterfly(
        local_lse, src_weight.reshape(own_clusters, CLUSTER), "key", key_size, key_index
    )
    group_dual = ENTROPY * jnp.log(group_weight) - ENTROPY * group_lse
    share_start = key_index * own_clusters
    src_dual = lax.dynamic_slice_in_dim(group_dual, share_start, own_clusters, 0).reshape(-1)

    tgt_shape = jax.ShapeDtypeStruct((tgt_clusters, CLUSTER), jnp.float32)
    column = pltpu.VMEM((tgt_clusters * CLUSTER, 128), jnp.float32)
    (tgt_part,) = _sweep(
        _second_kernel, (tgt_shape,), [column, column], ids, cnt, group_src, tgt_desc, sq_src, sq_tgt, group_dual
    )
    parts = lax.all_gather(tgt_part, "group", axis=0)
    merged = parts[0]
    for index in range(1, parts.shape[0]):
        merged = merge_lse(merged, parts[index])
    tgt_lse = merged.reshape(-1)
    tgt_dual_new = ENTROPY * jnp.log(tgt_weight) - ENTROPY * tgt_lse
    return (src_dual, tgt_dual_new)


def solution(mesh):
    in_specs = (
        P(("group", "key"), None),
        P("key", None),
        P(("group", "key")),
        P("key"),
        P("key"),
        P("group", "key", None, None),
        P("group", "key"),
    )
    out_specs = (P(("group", "key")), P("key"))
    return jax.shard_map(local, mesh=mesh, in_specs=in_specs, out_specs=out_specs, check_vma=False)
```

```python
import functools

import jax
import jax.numpy as jnp
from jax import lax
from jax.experimental import pallas as pl
from jax.experimental.pallas import tpu as pltpu
from jax.sharding import PartitionSpec as P

CLUSTER = 256
UNROLL = 4

ENTROPY = 0.05
INV_ENTROPY = 20.0
NEG_FLOOR = -1e30


def _slot_ids(ids_ref, slot, src_clusters, tgt_clusters):
    src_id = jnp.minimum(jnp.maximum(ids_ref[0, slot], 0), src_clusters - 1)
    tgt_id = jnp.minimum(jnp.maximum(ids_ref[1, slot], 0), tgt_clusters - 1)
    return src_id, tgt_id


def _block_cost(src_ref, tgt_ref, sqs_ref, sqt_ref, src_id, tgt_id, width):
    src_start = pl.multiple_of(src_id * CLUSTER, CLUSTER)
    tgt_start = pl.multiple_of(tgt_id * CLUSTER, CLUSTER)
    src_rows = src_ref[pl.ds(src_start, CLUSTER), :]
    tgt_rows = tgt_ref[pl.ds(tgt_start, CLUSTER), :]
    inner = lax.dot_general(
        tgt_rows, src_rows, (((1,), (1,)), ((), ())), preferred_element_type=jnp.float32
    )
    sq_s = sqs_ref[pl.ds(src_id, 1), :]
    sq_t = sqt_ref[pl.ds(tgt_start, CLUSTER), :]
    return (sq_s + sq_t) - (2.0 / width) * inner


def _first_kernel(ids_ref, cnt_ref, src_ref, tgt_ref, sqt_ref, pot_ref, top_ref, sqs_ref, tot_ref):
    src_clusters = sqs_ref.shape[0]
    tgt_clusters = tgt_ref.shape[0] // CLUSTER
    width = src_ref.shape[1]

    def norms(cluster, carry):
        rows = src_ref[pl.ds(pl.multiple_of(cluster * CLUSTER, CLUSTER), CLUSTER), :].astype(jnp.float32)
        squares = rows * rows
        folded = squares[:, : width // 2] + squares[:, width // 2 :]
        sqs_ref[pl.ds(cluster, 1), :] = jnp.sum(jnp.transpose(folded), axis=0, keepdims=True) / width
        return carry

    lax.fori_loop(0, src_clusters, norms, 0)
    top_ref[...] = jnp.full(top_ref.shape, NEG_FLOOR, jnp.float32)
    tot_ref[...] = jnp.zeros(tot_ref.shape, jnp.float32)
    count = jnp.minimum(jnp.maximum(cnt_ref[0], 0), ids_ref.shape[1])

    def scores_of(slot):
        src_id, tgt_id = _slot_ids(ids_ref, slot, src_clusters, tgt_clusters)
        cost = _block_cost(src_ref, tgt_ref, sqs_ref, sqt_ref, src_id, tgt_id, width)
        pot = pot_ref[pl.ds(pl.multiple_of(tgt_id * CLUSTER, CLUSTER), CLUSTER), :]
        return src_id, (pot - cost) * INV_ENTROPY

    def update(src_id, scores):
        peak = jnp.max(scores, axis=0, keepdims=True)
        old_top = top_ref[pl.ds(src_id, 1), :]
        old_tot = tot_ref[pl.ds(src_id, 1), :]
        new_top = jnp.maximum(old_top, peak)
        new_tot = old_tot * jnp.exp(old_top - new_top) + jnp.sum(
            jnp.exp(scores - new_top), axis=0, keepdims=True
        )
        top_ref[pl.ds(src_id, 1), :] = new_top
        tot_ref[pl.ds(src_id, 1), :] = new_tot

    def body(trip, carry):
        blocks = [scores_of(UNROLL * trip + lane) for lane in range(UNROLL)]
        for block in blocks:
            update(*block)
        return carry

    def tail(slot, carry):
        update(*scores_of(slot))
        return carry

    lax.fori_loop(0, count // UNROLL, body, 0)
    lax.fori_loop(count // UNROLL * UNROLL, count, tail, 0)
    top_ref[...] = jnp.maximum(top_ref[...] + jnp.log(tot_ref[...]), NEG_FLOOR)


def _second_kernel(ids_ref, cnt_ref, src_ref, tgt_ref, sqs_ref, sqt_ref, dual_ref, lse_ref, top_ref, tot_ref):
    src_clusters = sqs_ref.shape[0]
    tgt_clusters = tgt_ref.shape[0] // CLUSTER
    width = src_ref.shape[1]
    lanes = top_ref.shape[1]
    top_ref[...] = jnp.full(top_ref.shape, NEG_FLOOR, jnp.float32)
    tot_ref[...] = jnp.zeros(tot_ref.shape, jnp.float32)
    count = jnp.minimum(jnp.maximum(cnt_ref[0], 0), ids_ref.shape[1])

    def scores_of(slot):
        src_id, tgt_id = _slot_ids(ids_ref, slot, src_clusters, tgt_clusters)
        cost = _block_cost(src_ref, tgt_ref, sqs_ref, sqt_ref, src_id, tgt_id, width)
        pot = dual_ref[pl.ds(src_id, 1), :]
        return tgt_id, (pot - cost) * INV_ENTROPY

    def update(tgt_id, scores):
        halves = [scores[:, part * lanes:(part + 1) * lanes] for part in range(CLUSTER // lanes)]
        tgt_rows = pl.ds(pl.multiple_of(tgt_id * CLUSTER, CLUSTER), CLUSTER)
        old_top = top_ref[tgt_rows, :]
        old_tot = tot_ref[tgt_rows, :]
        new_top = old_top
        for half in halves:
            new_top = jnp.maximum(new_top, half)
        new_tot = old_tot * jnp.exp(old_top - new_top)
        for half in halves:
            new_tot = new_tot + jnp.exp(half - new_top)
        top_ref[tgt_rows, :] = new_top
        tot_ref[tgt_rows, :] = new_tot

    def body(trip, carry):
        blocks = [scores_of(UNROLL * trip + lane) for lane in range(UNROLL)]
        for block in blocks:
            update(*block)
        return carry

    def tail(slot, carry):
        update(*scores_of(slot))
        return carry

    lax.fori_loop(0, count // UNROLL, body, 0)
    lax.fori_loop(count // UNROLL * UNROLL, count, tail, 0)
    for cluster in range(tgt_clusters):
        rows = pl.ds(cluster * CLUSTER, CLUSTER)
        lane_top = top_ref[rows, :]
        peak = jnp.max(lane_top, axis=1, keepdims=True)
        total = jnp.sum(tot_ref[rows, :] * jnp.exp(lane_top - peak), axis=1, keepdims=True)
        column = jnp.maximum(peak + jnp.log(total), NEG_FLOOR)
        wide = jnp.broadcast_to(column, (CLUSTER, 128))
        lse_ref[pl.ds(cluster, 1), :] = jnp.transpose(wide)[0:1, :]


def _sweep(kernel, out_shapes, scratch, *operands):
    vmem = pl.BlockSpec(memory_space=pltpu.VMEM)
    smem = pl.BlockSpec(memory_space=pltpu.SMEM)
    ids, _, group_src, tgt_desc = operands[:4]
    slots = ids.shape[1]
    flops = 2 * slots * CLUSTER * CLUSTER * group_src.shape[1]
    return pl.pallas_call(
        kernel,
        out_shape=out_shapes,
        in_specs=[smem, smem] + [vmem] * (len(operands) - 2),
        out_specs=tuple(vmem for _ in out_shapes),
        scratch_shapes=scratch,
        compiler_params=pltpu.CompilerParams(vmem_limit_bytes=48 * 1024 * 1024),
        cost_estimate=pl.CostEstimate(
            flops=flops,
            transcendentals=slots * CLUSTER * CLUSTER,
            bytes_accessed=group_src.size * 2 + tgt_desc.size * 2,
        ),
    )(*operands)


def merge_lse(first, second):
    top = jnp.maximum(first, second)
    return top + jnp.log1p(jnp.exp(jnp.minimum(first, second) - top))


def butterfly(lse, weight, axis, size, index):
    bit = 1
    rows = lse.shape[0]
    while bit < size:
        perm = [(i, i ^ bit) for i in range(size)]
        other = lax.ppermute(jnp.concatenate([lse, weight], axis=0), axis, perm)
        lse = merge_lse(lse, other[:rows])
        is_low = (index & bit) == 0
        low = jnp.where(is_low, weight, other[rows:])
        high = jnp.where(is_low, other[rows:], weight)
        weight = jnp.concatenate([low, high], axis=0)
        bit *= 2
    return lse, weight


def local(src_desc, tgt_desc, src_weight, tgt_weight, tgt_dual, pair_blocks, pair_count):
    width = src_desc.shape[1]
    own_clusters = src_desc.shape[0] // CLUSTER
    key_size = lax.axis_size("key")
    src_clusters = own_clusters * key_size
    tgt_clusters = tgt_desc.shape[0] // CLUSTER
    slot_total = pair_blocks.shape[3]
    ids = pair_blocks.reshape(2, slot_total)
    cnt = pair_count.reshape(1)

    group_src = lax.all_gather(src_desc, "key", axis=0, tiled=True)

    sq_tgt = (jnp.sum(tgt_desc.astype(jnp.float32) ** 2, axis=1) / width).reshape(-1, 1)
    pot_col = tgt_dual.reshape(-1, 1)

    src_shape = jax.ShapeDtypeStruct((src_clusters, CLUSTER), jnp.float32)
    local_lse, sq_src = _sweep(
        _first_kernel, (src_shape, src_shape), [pltpu.VMEM((src_clusters, CLUSTER), jnp.float32)],
        ids, cnt, group_src, tgt_desc, sq_tgt, pot_col,
    )
    key_index = lax.axis_index("key")
    group_lse, group_weight = butterfly(
        local_lse, src_weight.reshape(own_clusters, CLUSTER), "key", key_size, key_index
    )
    group_dual = ENTROPY * jnp.log(group_weight) - ENTROPY * group_lse
    share_start = key_index * own_clusters
    src_dual = lax.dynamic_slice_in_dim(group_dual, share_start, own_clusters, 0).reshape(-1)

    tgt_shape = jax.ShapeDtypeStruct((tgt_clusters, CLUSTER), jnp.float32)
    column = pltpu.VMEM((tgt_clusters * CLUSTER, 128), jnp.float32)
    (tgt_part,) = _sweep(
        _second_kernel, (tgt_shape,), [column, column], ids, cnt, group_src, tgt_desc, sq_src, sq_tgt, group_dual
    )
    parts = lax.all_gather(tgt_part, "group", axis=0)
    merged = parts[0]
    for index in range(1, parts.shape[0]):
        merged = merge_lse(merged, parts[index])
    tgt_lse = merged.reshape(-1)
    tgt_dual_new = ENTROPY * jnp.log(tgt_weight) - ENTROPY * tgt_lse
    return (src_dual, tgt_dual_new)


def solution(mesh):
    in_specs = (
        P(("group", "key"), None),
        P("key", None),
        P(("group", "key")),
        P("key"),
        P("key"),
        P("group", "key", None, None),
        P("group", "key"),
    )
    out_specs = (P(("group", "key")), P("key"))
    return jax.shard_map(local, mesh=mesh, in_specs=in_specs, out_specs=out_specs, check_vma=False)
```

```python
import functools

import jax
import jax.numpy as jnp
from jax import lax
from jax.experimental import pallas as pl
from jax.experimental.pallas import tpu as pltpu
from jax.sharding import PartitionSpec as P

CLUSTER = 256
UNROLL = 8

ENTROPY = 0.05
INV_ENTROPY = 20.0
NEG_FLOOR = -1e30


def _slot_ids(ids_ref, slot, src_clusters, tgt_clusters):
    src_id = jnp.minimum(jnp.maximum(ids_ref[0, slot], 0), src_clusters - 1)
    tgt_id = jnp.minimum(jnp.maximum(ids_ref[1, slot], 0), tgt_clusters - 1)
    return src_id, tgt_id


def _block_cost(src_ref, tgt_ref, sqs_ref, sqt_ref, src_id, tgt_id, width):
    src_start = pl.multiple_of(src_id * CLUSTER, CLUSTER)
    tgt_start = pl.multiple_of(tgt_id * CLUSTER, CLUSTER)
    src_rows = src_ref[pl.ds(src_start, CLUSTER), :]
    tgt_rows = tgt_ref[pl.ds(tgt_start, CLUSTER), :]
    inner = lax.dot_general(
        tgt_rows, src_rows, (((1,), (1,)), ((), ())), preferred_element_type=jnp.float32
    )
    sq_s = sqs_ref[pl.ds(src_id, 1), :]
    sq_t = sqt_ref[pl.ds(tgt_start, CLUSTER), :]
    return (sq_s + sq_t) - (2.0 / width) * inner


def _first_kernel(ids_ref, cnt_ref, src_ref, tgt_ref, sqs_ref, sqt_ref, pot_ref, top_ref, tot_ref):
    src_clusters = sqs_ref.shape[0]
    tgt_clusters = tgt_ref.shape[0] // CLUSTER
    width = src_ref.shape[1]
    top_ref[...] = jnp.full(top_ref.shape, NEG_FLOOR, jnp.float32)
    tot_ref[...] = jnp.zeros(tot_ref.shape, jnp.float32)
    count = jnp.minimum(jnp.maximum(cnt_ref[0], 0), ids_ref.shape[1])

    def scores_of(slot):
        src_id, tgt_id = _slot_ids(ids_ref, slot, src_clusters, tgt_clusters)
        cost = _block_cost(src_ref, tgt_ref, sqs_ref, sqt_ref, src_id, tgt_id, width)
        pot = pot_ref[pl.ds(pl.multiple_of(tgt_id * CLUSTER, CLUSTER), CLUSTER), :]
        return src_id, (pot - cost) * INV_ENTROPY

    def update(src_id, scores):
        peak = jnp.max(scores, axis=0, keepdims=True)
        old_top = top_ref[pl.ds(src_id, 1), :]
        old_tot = tot_ref[pl.ds(src_id, 1), :]
        new_top = jnp.maximum(old_top, peak)
        new_tot = old_tot * jnp.exp(old_top - new_top) + jnp.sum(
            jnp.exp(scores - new_top), axis=0, keepdims=True
        )
        top_ref[pl.ds(src_id, 1), :] = new_top
        tot_ref[pl.ds(src_id, 1), :] = new_tot

    def body(trip, carry):
        blocks = [scores_of(UNROLL * trip + lane) for lane in range(UNROLL)]
        for block in blocks:
            update(*block)
        return carry

    def tail(slot, carry):
        update(*scores_of(slot))
        return carry

    lax.fori_loop(0, count // UNROLL, body, 0)
    lax.fori_loop(count // UNROLL * UNROLL, count, tail, 0)
    top_ref[...] = jnp.maximum(top_ref[...] + jnp.log(tot_ref[...]), NEG_FLOOR)


def _second_kernel(ids_ref, cnt_ref, src_ref, tgt_ref, sqs_ref, sqt_ref, dual_ref, lse_ref, top_ref, tot_ref):
    src_clusters = sqs_ref.shape[0]
    tgt_clusters = tgt_ref.shape[0] // CLUSTER
    width = src_ref.shape[1]
    lanes = top_ref.shape[1]
    top_ref[...] = jnp.full(top_ref.shape, NEG_FLOOR, jnp.float32)
    tot_ref[...] = jnp.zeros(tot_ref.shape, jnp.float32)
    count = jnp.minimum(jnp.maximum(cnt_ref[0], 0), ids_ref.shape[1])

    def scores_of(slot):
        src_id, tgt_id = _slot_ids(ids_ref, slot, src_clusters, tgt_clusters)
        cost = _block_cost(src_ref, tgt_ref, sqs_ref, sqt_ref, src_id, tgt_id, width)
        pot = dual_ref[pl.ds(src_id, 1), :]
        return tgt_id, (pot - cost) * INV_ENTROPY

    def update(tgt_id, scores):
        halves = [scores[:, part * lanes:(part + 1) * lanes] for part in range(CLUSTER // lanes)]
        tgt_rows = pl.ds(pl.multiple_of(tgt_id * CLUSTER, CLUSTER), CLUSTER)
        old_top = top_ref[tgt_rows, :]
        old_tot = tot_ref[tgt_rows, :]
        new_top = old_top
        for half in halves:
            new_top = jnp.maximum(new_top, half)
        new_tot = old_tot * jnp.exp(old_top - new_top)
        for half in halves:
            new_tot = new_tot + jnp.exp(half - new_top)
        top_ref[tgt_rows, :] = new_top
        tot_ref[tgt_rows, :] = new_tot

    def body(trip, carry):
        blocks = [scores_of(UNROLL * trip + lane) for lane in range(UNROLL)]
        for block in blocks:
            update(*block)
        return carry

    def tail(slot, carry):
        update(*scores_of(slot))
        return carry

    lax.fori_loop(0, count // UNROLL, body, 0)
    lax.fori_loop(count // UNROLL * UNROLL, count, tail, 0)
    for cluster in range(tgt_clusters):
        rows = pl.ds(cluster * CLUSTER, CLUSTER)
        lane_top = top_ref[rows, :]
        peak = jnp.max(lane_top, axis=1, keepdims=True)
        total = jnp.sum(tot_ref[rows, :] * jnp.exp(lane_top - peak), axis=1, keepdims=True)
        column = jnp.maximum(peak + jnp.log(total), NEG_FLOOR)
        wide = jnp.broadcast_to(column, (CLUSTER, 128))
        lse_ref[pl.ds(cluster, 1), :] = jnp.transpose(wide)[0:1, :]


def _sweep(kernel, out_shapes, scratch, ids, cnt, group_src, tgt_desc, sq_src, sq_tgt, pot):
    vmem = pl.BlockSpec(memory_space=pltpu.VMEM)
    smem = pl.BlockSpec(memory_space=pltpu.SMEM)
    slots = ids.shape[1]
    flops = 2 * slots * CLUSTER * CLUSTER * group_src.shape[1]
    return pl.pallas_call(
        kernel,
        out_shape=out_shapes,
        in_specs=[smem, smem, vmem, vmem, vmem, vmem, vmem],
        out_specs=tuple(vmem for _ in out_shapes),
        scratch_shapes=scratch,
        compiler_params=pltpu.CompilerParams(vmem_limit_bytes=48 * 1024 * 1024),
        cost_estimate=pl.CostEstimate(
            flops=flops,
            transcendentals=slots * CLUSTER * CLUSTER,
            bytes_accessed=group_src.size * 2 + tgt_desc.size * 2,
        ),
    )(ids, cnt, group_src, tgt_desc, sq_src, sq_tgt, pot)


def merge_lse(first, second):
    top = jnp.maximum(first, second)
    return top + jnp.log1p(jnp.exp(jnp.minimum(first, second) - top))


def butterfly(lse, weight, axis, size, index):
    bit = 1
    rows = lse.shape[0]
    while bit < size:
        perm = [(i, i ^ bit) for i in range(size)]
        other = lax.ppermute(jnp.concatenate([lse, weight], axis=0), axis, perm)
        lse = merge_lse(lse, other[:rows])
        is_low = (index & bit) == 0
        low = jnp.where(is_low, weight, other[rows:])
        high = jnp.where(is_low, other[rows:], weight)
        weight = jnp.concatenate([low, high], axis=0)
        bit *= 2
    return lse, weight


def local(src_desc, tgt_desc, src_weight, tgt_weight, tgt_dual, pair_blocks, pair_count):
    width = src_desc.shape[1]
    own_clusters = src_desc.shape[0] // CLUSTER
    key_size = lax.axis_size("key")
    src_clusters = own_clusters * key_size
    tgt_clusters = tgt_desc.shape[0] // CLUSTER
    slot_total = pair_blocks.shape[3]
    ids = pair_blocks.reshape(2, slot_total)
    cnt = pair_count.reshape(1)

    group_src = lax.all_gather(src_desc, "key", axis=0, tiled=True)
    sq_src = (jnp.sum(group_src.astype(jnp.float32) ** 2, axis=1) / width).reshape(src_clusters, CLUSTER)

    sq_tgt = (jnp.sum(tgt_desc.astype(jnp.float32) ** 2, axis=1) / width).reshape(-1, 1)
    pot_col = tgt_dual.reshape(-1, 1)

    src_shape = jax.ShapeDtypeStruct((src_clusters, CLUSTER), jnp.float32)
    local_lse, _ = _sweep(
        _first_kernel, (src_shape, src_shape), [], ids, cnt, group_src, tgt_desc, sq_src, sq_tgt, pot_col
    )
    key_index = lax.axis_index("key")
    group_lse, group_weight = butterfly(
        local_lse, src_weight.reshape(own_clusters, CLUSTER), "key", key_size, key_index
    )
    group_dual = ENTROPY * jnp.log(group_weight) - ENTROPY * group_lse
    share_start = key_index * own_clusters
    src_dual = lax.dynamic_slice_in_dim(group_dual, share_start, own_clusters, 0).reshape(-1)

    tgt_shape = jax.ShapeDtypeStruct((tgt_clusters, CLUSTER), jnp.float32)
    column = pltpu.VMEM((tgt_clusters * CLUSTER, 128), jnp.float32)
    (tgt_part,) = _sweep(
        _second_kernel, (tgt_shape,), [column, column], ids, cnt, group_src, tgt_desc, sq_src, sq_tgt, group_dual
    )
    parts = lax.all_gather(tgt_part, "group", axis=0)
    merged = parts[0]
    for index in range(1, parts.shape[0]):
        merged = merge_lse(merged, parts[index])
    tgt_lse = merged.reshape(-1)
    tgt_dual_new = ENTROPY * jnp.log(tgt_weight) - ENTROPY * tgt_lse
    return (src_dual, tgt_dual_new)


def solution(mesh):
    in_specs = (
        P(("group", "key"), None),
        P("key", None),
        P(("group", "key")),
        P("key"),
        P("key"),
        P("group", "key", None, None),
        P("group", "key"),
    )
    out_specs = (P(("group", "key")), P("key"))
    return jax.shard_map(local, mesh=mesh, in_specs=in_specs, out_specs=out_specs, check_vma=False)
```

```python
import functools

import jax
import jax.numpy as jnp
from jax import lax
from jax.experimental import pallas as pl
from jax.experimental.pallas import tpu as pltpu
from jax.sharding import PartitionSpec as P

CLUSTER = 256
UNROLL = 8

ENTROPY = 0.05
INV_ENTROPY = 20.0
NEG_FLOOR = -1e30


def _slot_ids(ids_ref, slot, src_clusters, tgt_clusters):
    src_id = jnp.minimum(jnp.maximum(ids_ref[0, slot], 0), src_clusters - 1)
    tgt_id = jnp.minimum(jnp.maximum(ids_ref[1, slot], 0), tgt_clusters - 1)
    return src_id, tgt_id


def _block_cost(src_ref, tgt_ref, sqs_ref, sqt_ref, src_id, tgt_id, width):
    src_start = pl.multiple_of(src_id * CLUSTER, CLUSTER)
    tgt_start = pl.multiple_of(tgt_id * CLUSTER, CLUSTER)
    src_rows = src_ref[pl.ds(src_start, CLUSTER), :]
    tgt_rows = tgt_ref[pl.ds(tgt_start, CLUSTER), :]
    inner = lax.dot_general(
        tgt_rows, src_rows, (((1,), (1,)), ((), ())), preferred_element_type=jnp.float32
    )
    sq_s = sqs_ref[pl.ds(src_id, 1), :]
    sq_t = sqt_ref[pl.ds(tgt_start, CLUSTER), :]
    return (sq_s + sq_t) - (2.0 / width) * inner


def _first_kernel(ids_ref, cnt_ref, src_ref, tgt_ref, sqs_ref, sqt_ref, pot_ref, top_ref, tot_ref):
    src_clusters = sqs_ref.shape[0]
    tgt_clusters = tgt_ref.shape[0] // CLUSTER
    width = src_ref.shape[1]
    top_ref[...] = jnp.full(top_ref.shape, NEG_FLOOR, jnp.float32)
    tot_ref[...] = jnp.zeros(tot_ref.shape, jnp.float32)
    count = jnp.minimum(jnp.maximum(cnt_ref[0], 0), ids_ref.shape[1])

    def scores_of(slot):
        src_id, tgt_id = _slot_ids(ids_ref, slot, src_clusters, tgt_clusters)
        cost = _block_cost(src_ref, tgt_ref, sqs_ref, sqt_ref, src_id, tgt_id, width)
        pot = pot_ref[pl.ds(pl.multiple_of(tgt_id * CLUSTER, CLUSTER), CLUSTER), :]
        return src_id, (pot - cost) * INV_ENTROPY

    def update(src_id, scores):
        peak = jnp.max(scores, axis=0, keepdims=True)
        old_top = top_ref[pl.ds(src_id, 1), :]
        old_tot = tot_ref[pl.ds(src_id, 1), :]
        new_top = jnp.maximum(old_top, peak)
        new_tot = old_tot * jnp.exp(old_top - new_top) + jnp.sum(
            jnp.exp(scores - new_top), axis=0, keepdims=True
        )
        top_ref[pl.ds(src_id, 1), :] = new_top
        tot_ref[pl.ds(src_id, 1), :] = new_tot

    def body(trip, carry):
        blocks = [scores_of(UNROLL * trip + lane) for lane in range(UNROLL)]
        for block in blocks:
            update(*block)
        return carry

    def tail(slot, carry):
        update(*scores_of(slot))
        return carry

    lax.fori_loop(0, count // UNROLL, body, 0)
    lax.fori_loop(count // UNROLL * UNROLL, count, tail, 0)
    top_ref[...] = jnp.maximum(top_ref[...] + jnp.log(tot_ref[...]), NEG_FLOOR)


def _second_kernel(ids_ref, cnt_ref, src_ref, tgt_ref, sqs_ref, sqt_ref, dual_ref, lse_ref, top_ref, tot_ref):
    src_clusters = sqs_ref.shape[0]
    tgt_clusters = tgt_ref.shape[0] // CLUSTER
    width = src_ref.shape[1]
    lanes = top_ref.shape[1]
    top_ref[...] = jnp.full(top_ref.shape, NEG_FLOOR, jnp.float32)
    tot_ref[...] = jnp.zeros(tot_ref.shape, jnp.float32)
    count = jnp.minimum(jnp.maximum(cnt_ref[0], 0), ids_ref.shape[1])

    def scores_of(slot):
        src_id, tgt_id = _slot_ids(ids_ref, slot, src_clusters, tgt_clusters)
        cost = _block_cost(src_ref, tgt_ref, sqs_ref, sqt_ref, src_id, tgt_id, width)
        pot = dual_ref[pl.ds(src_id, 1), :]
        return tgt_id, (pot - cost) * INV_ENTROPY

    def update(tgt_id, scores):
        halves = [scores[:, part * lanes:(part + 1) * lanes] for part in range(CLUSTER // lanes)]
        tgt_rows = pl.ds(pl.multiple_of(tgt_id * CLUSTER, CLUSTER), CLUSTER)
        old_top = top_ref[tgt_rows, :]
        old_tot = tot_ref[tgt_rows, :]
        new_top = old_top
        for half in halves:
            new_top = jnp.maximum(new_top, half)
        new_tot = old_tot * jnp.exp(old_top - new_top)
        for half in halves:
            new_tot = new_tot + jnp.exp(half - new_top)
        top_ref[tgt_rows, :] = new_top
        tot_ref[tgt_rows, :] = new_tot

    def body(trip, carry):
        blocks = [scores_of(UNROLL * trip + lane) for lane in range(UNROLL)]
        for block in blocks:
            update(*block)
        return carry

    def tail(slot, carry):
        update(*scores_of(slot))
        return carry

    lax.fori_loop(0, count // UNROLL, body, 0)
    lax.fori_loop(count // UNROLL * UNROLL, count, tail, 0)
    for cluster in range(tgt_clusters):
        rows = pl.ds(cluster * CLUSTER, CLUSTER)
        lane_top = top_ref[rows, :]
        peak = jnp.max(lane_top, axis=1, keepdims=True)
        total = jnp.sum(tot_ref[rows, :] * jnp.exp(lane_top - peak), axis=1, keepdims=True)
        column = jnp.maximum(peak + jnp.log(total), NEG_FLOOR)
        wide = jnp.broadcast_to(column, (CLUSTER, 128))
        lse_ref[pl.ds(cluster, 1), :] = jnp.transpose(wide)[0:1, :]


def _sweep(kernel, out_shapes, scratch, ids, cnt, group_src, tgt_desc, sq_src, sq_tgt, pot):
    vmem = pl.BlockSpec(memory_space=pltpu.VMEM)
    smem = pl.BlockSpec(memory_space=pltpu.SMEM)
    slots = ids.shape[1]
    flops = 2 * slots * CLUSTER * CLUSTER * group_src.shape[1]
    return pl.pallas_call(
        kernel,
        out_shape=out_shapes,
        in_specs=[smem, smem, vmem, vmem, vmem, vmem, vmem],
        out_specs=tuple(vmem for _ in out_shapes),
        scratch_shapes=scratch,
        compiler_params=pltpu.CompilerParams(vmem_limit_bytes=48 * 1024 * 1024),
        cost_estimate=pl.CostEstimate(
            flops=flops,
            transcendentals=slots * CLUSTER * CLUSTER,
            bytes_accessed=group_src.size * 2 + tgt_desc.size * 2,
        ),
    )(ids, cnt, group_src, tgt_desc, sq_src, sq_tgt, pot)


def merge_lse(first, second):
    top = jnp.maximum(first, second)
    return top + jnp.log1p(jnp.exp(jnp.minimum(first, second) - top))


def butterfly(lse, weight, axis, size, index):
    rows = lse.shape[0]
    bits = []
    bit = 1
    while bit < size:
        bits.insert(0, bit)
        bit *= 2
    for bit in bits:
        perm = [(i, i ^ bit) for i in range(size)]
        other = lax.ppermute(jnp.concatenate([lse, weight], axis=0), axis, perm)
        lse = merge_lse(lse, other[:rows])
        is_low = (index & bit) == 0
        low = jnp.where(is_low, weight, other[rows:])
        high = jnp.where(is_low, other[rows:], weight)
        weight = jnp.concatenate([low, high], axis=0)
    width = len(bits)
    order = [int(format(c, "0%db" % width)[::-1], 2) if width else 0 for c in range(size)]
    units = weight.reshape(size, -1, weight.shape[-1])
    weight = jnp.take(units, jnp.array(order, jnp.int32), axis=0).reshape(weight.shape)
    return lse, weight


def local(src_desc, tgt_desc, src_weight, tgt_weight, tgt_dual, pair_blocks, pair_count):
    width = src_desc.shape[1]
    own_clusters = src_desc.shape[0] // CLUSTER
    key_size = lax.axis_size("key")
    src_clusters = own_clusters * key_size
    tgt_clusters = tgt_desc.shape[0] // CLUSTER
    slot_total = pair_blocks.shape[3]
    ids = pair_blocks.reshape(2, slot_total)
    cnt = pair_count.reshape(1)

    group_src = lax.all_gather(src_desc, "key", axis=0, tiled=True)
    sq_src = (jnp.sum(group_src.astype(jnp.float32) ** 2, axis=1) / width).reshape(src_clusters, CLUSTER)

    sq_tgt = (jnp.sum(tgt_desc.astype(jnp.float32) ** 2, axis=1) / width).reshape(-1, 1)
    pot_col = tgt_dual.reshape(-1, 1)

    src_shape = jax.ShapeDtypeStruct((src_clusters, CLUSTER), jnp.float32)
    local_lse, _ = _sweep(
        _first_kernel, (src_shape, src_shape), [], ids, cnt, group_src, tgt_desc, sq_src, sq_tgt, pot_col
    )
    key_index = lax.axis_index("key")
    group_lse, group_weight = butterfly(
        local_lse, src_weight.reshape(own_clusters, CLUSTER), "key", key_size, key_index
    )
    group_dual = ENTROPY * jnp.log(group_weight) - ENTROPY * group_lse
    share_start = key_index * own_clusters
    src_dual = lax.dynamic_slice_in_dim(group_dual, share_start, own_clusters, 0).reshape(-1)

    tgt_shape = jax.ShapeDtypeStruct((tgt_clusters, CLUSTER), jnp.float32)
    column = pltpu.VMEM((tgt_clusters * CLUSTER, 128), jnp.float32)
    (tgt_part,) = _sweep(
        _second_kernel, (tgt_shape,), [column, column], ids, cnt, group_src, tgt_desc, sq_src, sq_tgt, group_dual
    )
    parts = lax.all_gather(tgt_part, "group", axis=0)
    merged = parts[0]
    for index in range(1, parts.shape[0]):
        merged = merge_lse(merged, parts[index])
    tgt_lse = merged.reshape(-1)
    tgt_dual_new = ENTROPY * jnp.log(tgt_weight) - ENTROPY * tgt_lse
    return (src_dual, tgt_dual_new)


def solution(mesh):
    in_specs = (
        P(("group", "key"), None),
        P("key", None),
        P(("group", "key")),
        P("key"),
        P("key"),
        P("group", "key", None, None),
        P("group", "key"),
    )
    out_specs = (P(("group", "key")), P("key"))
    return jax.shard_map(local, mesh=mesh, in_specs=in_specs, out_specs=out_specs, check_vma=False)
```
